128 devices in a mesh: seq: 16 (over y_hi, x, core), head: 8 (over z, y_lo).
Axes of the slice: x: 4, y: 4 (y_hi: 2, y_lo: 2; y = y_hi * 2 + y_lo), z: 4, core: 2. Of those that a mesh axis runs over, the one named last changes fastest.
Arguments:
- inputs_x: bfloat16 [4096, 8192], P('seq', 'head'), may hold values from -6 to 6
- inputs_b: bfloat16 [4096, 1024], P('seq', 'head'), may hold values from -0.59765625 to 0.59765625
- inputs_c: bfloat16 [4096, 1024], P('seq', 'head'), may hold values from -6 to 6
- gate_z: bfloat16 [4096, 8192], P('seq', 'head'), may hold values from -6 to 6
- log_decay: float32 [128, 4096], P('head', 'seq'), may hold values from -1 to 0, as said below
- resets: int32 [4096], P('seq'), may hold values from 0 to 1, as said below
- norm_gain: float32 [8192], P('head'), may hold values from 0.1 to 1.9
- out_weight: bfloat16 [4096, 8192], P('seq', 'head'), may hold values from -0.09375 to 0.09375
- out_grad: bfloat16 [4096, 4096], P('seq', 'head'), may hold values from -6 to 6
Outputs:
- layer_out: bfloat16 [4096, 4096], P('seq', 'head')
- grad_x: float32 [4096, 8192], P('seq', 'head')
- grad_b: float32 [4096, 1024], P('seq', 'head')
- grad_c: float32 [4096, 1024], P('seq', 'head')
- grad_z: float32 [4096, 8192], P('seq', 'head')
- grad_decay: float32 [128, 4096], P('head', 'seq')
- grad_weight: float32 [4096, 8192], P('seq', 'head')
The draws below stay inside these ranges and needn't reach their ends.
Inputs may be any that keep to these rules, and one draw needn't show every extreme that they name: `log_decay`: the decay factor of a token is exp of its entry. `resets`: exactly one entry is 1, the first token of the second rollout, at a position from 512 to 3583.
All inputs are finite; a program needn't handle non-finite values.
Results may differ from the reference program's by a relative error of at most 0.023.
Values may be sent and summed in bfloat16 or wider, within the bound.
No kernel may reach another device: no remote copies, remote signals or barrier semaphores. Data moves between devices by JAX's collectives and lax.ppermute only.
A program may use at most 128 MiB of HBM per device.

```python
import jax
import jax.numpy as jnp
from jax import lax

D = 4096
SSD_HALF_LANES = 128
P_SIZE = 64
N = 128
G = 8
SPAN = 256
TOK_DEV = 256
DIALOGUE_SYMBOLS = 4096
HP = 8192
N_SEQ = 16
N_HEAD = 8


def draw_resets(key, part):
    position = jax.random.randint(key, (), DIALOGUE_SYMBOLS // 8, DIALOGUE_SYMBOLS - DIALOGUE_SYMBOLS // 8)
    return (jnp.arange(DIALOGUE_SYMBOLS, dtype=jnp.int32) == position).astype(jnp.int32)


def draw_log_decay(key, part):
    sampler_seeds = jax.random.split(key, 7)
    slow_share = 0.5
    slow = jax.random.uniform(sampler_seeds[0], (SSD_HALF_LANES, 1)) < slow_share
    slow_rate = jax.random.uniform(sampler_seeds[1], (SSD_HALF_LANES, 1), minval=0.3, maxval=1.0) / DIALOGUE_SYMBOLS
    fast_rate = jax.random.uniform(sampler_seeds[2], (SSD_HALF_LANES, 1), minval=0.02, maxval=0.035)
    starting_displacement = jnp.where(slow, slow_rate, fast_rate)
    approximate_guess = jnp.exp(jax.random.uniform(sampler_seeds[3], (SSD_HALF_LANES, DIALOGUE_SYMBOLS), minval=-0.69, maxval=0.69))
    block_count = DIALOGUE_SYMBOLS // TOK_DEV
    segment_multiplier = jnp.exp(jax.random.uniform(sampler_seeds[4], (SSD_HALF_LANES, block_count, 1), minval=-0.69, maxval=0.69))
    segment_multiplier = jnp.broadcast_to(segment_multiplier, (SSD_HALF_LANES, block_count, TOK_DEV)).reshape(SSD_HALF_LANES, DIALOGUE_SYMBOLS)
    segment_number = jax.random.uniform(sampler_seeds[5], (SSD_HALF_LANES, DIALOGUE_SYMBOLS)) < 2.0 / DIALOGUE_SYMBOLS
    segment_extent = jax.random.uniform(sampler_seeds[6], (SSD_HALF_LANES, DIALOGUE_SYMBOLS), minval=0.22, maxval=0.69)
    return (-(starting_displacement * approximate_guess * segment_multiplier + jnp.where(segment_number, segment_extent, 0.0))).astype(jnp.float32)


def with_spikes(array, rng, source, target, shards_of, factor):
    def block_of(axis_at):
        return (jnp.arange(array.shape[axis_at]) // (array.shape[axis_at] // shards_of)).reshape((-1,) + (1,) * (array.ndim - 1 - axis_at))

    one_side = jax.random.permutation(rng, shards_of)[block_of(target)]
    far = (block_of(target) + shards_of // 2) % shards_of
    return jnp.where((block_of(source) == one_side) | (block_of(source) == far), factor * array, array)


def shard_levels(rng, shape, cuts, smallest, top_value):
    def one(dim, parts):
        draws = jax.random.uniform(jax.random.fold_in(jax.random.fold_in(rng, 6), dim), (parts,), jnp.float32, smallest / len(cuts), top_value / len(cuts))
        return jnp.repeat(jnp.exp(draws), shape[dim] // parts).reshape((-1,) + (1,) * (len(shape) - dim - 1))

    level = one(*cuts[0])
    for cut in cuts[1:]:
        level = level * one(*cut)
    return level


def gaussian(rng, dims, scale, bound, shards=(), kind=jnp.bfloat16):
    entries = scale * jax.random.normal(rng, dims, jnp.float32)
    if shards:
        entries = entries * shard_levels(rng, dims, shards, -0.22, 0.18)
    return jnp.clip(entries, -bound, bound).astype(kind)


def heavy_noise(rng, extent, scale, limit, cuts, heavy, kind=jnp.bfloat16):
    values = scale * jax.random.normal(rng, extent, jnp.float32)
    if cuts:
        values = values * shard_levels(rng, extent, cuts, -0.22, 0.18)
    return jnp.clip(with_spikes(values, jax.random.fold_in(rng, 3), *heavy), -limit, limit).astype(kind)


def setup_inputs(seed: int = 0) -> dict:
    key_of = jax.random.split(jax.random.key(seed), 10)
    inputs_x = gaussian(key_of[0], (DIALOGUE_SYMBOLS, HP), 1.0, 6.0, ((0, 16), (1, 8)))
    inputs_b = gaussian(key_of[1], (DIALOGUE_SYMBOLS, G * N), 0.1, 0.59765625, ((0, 16), (1, 8)))
    inputs_c = gaussian(key_of[2], (DIALOGUE_SYMBOLS, G * N), 1.0, 6.0, ((0, 16), (1, 8)))
    gate_z = gaussian(key_of[3], (DIALOGUE_SYMBOLS, HP), 1.0, 6.0, ((0, 16), (1, 8)))
    log_decay = draw_log_decay(jax.random.fold_in(key_of[9], 71), 0)
    resets = draw_resets(jax.random.fold_in(key_of[9], 71), 0)
    norm_gain = jnp.clip(1.0 + 0.18 * jax.random.normal(key_of[6], (HP,), jnp.float32), 0.1, 1.9)
    out_weight = heavy_noise(key_of[7], (D, HP), HP ** -0.5, 0.09375, ((0, 16), (1, 8)), (1, 0, 16, 2.0))
    out_grad = heavy_noise(key_of[8], (DIALOGUE_SYMBOLS, D), 1.0, 6.0, ((0, 16), (1, 8)), (0, 1, 16, 2.0))
    return dict(inputs_x=inputs_x, inputs_b=inputs_b, inputs_c=inputs_c, gate_z=gate_z, log_decay=log_decay, resets=resets, norm_gain=norm_gain, out_weight=out_weight, out_grad=out_grad)


def span_scan(inputs_x, inputs_b, inputs_c, log_decay, resets, start_state):
    tokens_here = inputs_x.shape[0]
    heads_here = log_decay.shape[0]
    groups_here = inputs_b.shape[1] // N
    repeat_count = heads_here // groups_here
    blocks = tokens_here // SPAN
    x_blocks = inputs_x.reshape(blocks, SPAN, heads_here, P_SIZE)
    b_blocks = inputs_b.reshape(blocks, SPAN, groups_here, N)
    c_blocks = inputs_c.reshape(blocks, SPAN, groups_here, N)
    d_blocks = log_decay.reshape(heads_here, blocks, SPAN).transpose(1, 0, 2)
    r_blocks = resets.reshape(blocks, SPAN)
    order = jnp.arange(SPAN, dtype=jnp.int32)
    lower = order[None, :] <= order[:, None]

    def advance(state, pieces):
        x_here, b_here, c_here, d_here, r_here = pieces
        cumul = jnp.cumsum(d_here, axis=1)
        counts = jnp.cumsum(r_here)
        same = lower & (counts[:, None] == counts[None, :])
        spread = cumul[:, :, None] - cumul[:, None, :]
        weights = jnp.where(same[None], jnp.exp(jnp.minimum(spread, 0.0)), 0.0)
        scores = jnp.einsum('tgn,sgn->gts', c_here, b_here, precision=lax.Precision.HIGHEST)
        scores = jnp.repeat(scores, repeat_count, axis=0) * weights
        inner = jnp.einsum('hts,shp->thp', scores, x_here, precision=lax.Precision.HIGHEST)
        c_heads = jnp.repeat(c_here, repeat_count, axis=1)
        b_heads = jnp.repeat(b_here, repeat_count, axis=1)
        entry = jnp.exp(cumul) * (counts == 0).astype(jnp.float32)[None, :]
        carried = jnp.einsum('thn,hpn->thp', c_heads, state, precision=lax.Precision.HIGHEST) * entry.T[:, :, None]
        tail = jnp.exp(cumul[:, -1:] - cumul) * (counts == counts[-1]).astype(jnp.float32)[None, :]
        fresh = jnp.einsum('shp,shn->hpn', x_here * tail.T[:, :, None], b_heads, precision=lax.Precision.HIGHEST)
        passing = entry[:, -1]
        return (fresh + passing[:, None, None] * state, inner + carried)
    final, outputs = lax.scan(jax.checkpoint(advance), start_state, (x_blocks, b_blocks, c_blocks, d_blocks, r_blocks))
    return (outputs.reshape(tokens_here, heads_here * P_SIZE), final)

def gated_norm(values, gate, gain):
    gated = values * jax.nn.silu(gate)
    rows_here, width = gated.shape
    group_width = HP // G
    grouped = gated.reshape(rows_here, width // group_width, group_width)
    scale = lax.rsqrt(lax.optimization_barrier(jnp.mean(grouped * grouped, axis=2, keepdims=True)) + 1e-05)
    return (grouped * scale).reshape(rows_here, width) * gain[None, :]

def reference(inputs_x, inputs_b, inputs_c, gate_z, log_decay, resets, norm_gain, out_weight, out_grad):
    start_state = jnp.zeros((SSD_HALF_LANES, P_SIZE, N), jnp.float32)

    def forward(x_float, b_float, c_float, z_float, decay_arg):
        values, unused_final = span_scan(x_float, b_float, c_float, decay_arg, resets, start_state)
        return gated_norm(values, z_float, norm_gain)
    normed, pullback = jax.vjp(forward, inputs_x.astype(jnp.float32), inputs_b.astype(jnp.float32), inputs_c.astype(jnp.float32), gate_z.astype(jnp.float32), log_decay)
    normed_bf = normed.astype(jnp.bfloat16)
    width_dev = HP // N_HEAD
    total = jnp.zeros((DIALOGUE_SYMBOLS, D), jnp.float32)
    for shard_index in range(N_HEAD):
        low = shard_index * width_dev
        part_term = lax.dot_general(normed_bf[:, low:low + width_dev], out_weight[:, low:low + width_dev], (((1,), (1,)), ((), ())), preferred_element_type=jnp.float32)
        total = total + lax.optimization_barrier(part_term.astype(jnp.bfloat16)).astype(jnp.float32)
    layer_out = total.astype(jnp.bfloat16)
    grad_y = jnp.dot(out_grad, out_weight, preferred_element_type=jnp.float32)
    grad_weight = jnp.zeros((D, HP), jnp.float32)
    for block_index in range(N_SEQ):
        low = block_index * TOK_DEV
        weight_term = lax.dot_general(out_grad[low:low + TOK_DEV], normed_bf[low:low + TOK_DEV], (((0,), (0,)), ((), ())), preferred_element_type=jnp.float32)
        grad_weight = grad_weight + lax.optimization_barrier(weight_term.astype(jnp.bfloat16)).astype(jnp.float32)
    grad_x, grad_b, grad_c, grad_z, grad_decay = pullback(grad_y)
    return (layer_out, grad_x, grad_b, grad_c, grad_z, grad_decay, grad_weight)
```

```python
import jax
import jax.numpy as jnp
from jax import lax
from jax.sharding import PartitionSpec as P

P_SIZE = 64
N = 128
G = 8
SPAN = 256
HP = 8192


def from_behind(value, axis, steps):
    count = lax.axis_size(axis)
    leading, last = (max(0, -steps), min(count, count - steps))
    return lax.ppermute(value, axis, [(source, source + steps) for source in range(leading, last)])


def prefix_combine(decay, value, direction):
    count = lax.axis_size("seq")

    def shifted(item, steps):
        return from_behind(item, "seq", direction * steps)

    def sent(item):
        return item.astype(jnp.bfloat16)

    near = shifted(sent(value), 1).astype(jnp.float32)
    total = near
    window_decay = shifted(decay, 1)
    window = 1
    if count > 2:
        far = shifted(sent(value), 2).astype(jnp.float32)
        total = near + window_decay[:, None, None] * far
        window_decay = window_decay * shifted(decay, 2)
        window = 2
    while window < count - 1:
        incoming = shifted(sent(total), window).astype(jnp.float32)
        next_decay = None
        if 2 * window < count - 1:
            next_decay = window_decay * shifted(window_decay, window)
        total = total + window_decay[:, None, None] * incoming
        window_decay = next_decay
        window *= 2
    return total


def span_scan(inputs_x, inputs_b, inputs_c, log_decay, resets, start_state):
    tokens_here = inputs_x.shape[0]
    heads_here = log_decay.shape[0]
    groups_here = inputs_b.shape[1] // N
    repeat_count = heads_here // groups_here
    blocks = tokens_here // SPAN
    x_blocks = inputs_x.reshape(blocks, SPAN, heads_here, P_SIZE)
    b_blocks = inputs_b.reshape(blocks, SPAN, groups_here, N)
    c_blocks = inputs_c.reshape(blocks, SPAN, groups_here, N)
    d_blocks = log_decay.reshape(heads_here, blocks, SPAN).transpose(1, 0, 2)
    r_blocks = resets.reshape(blocks, SPAN)
    order = jnp.arange(SPAN, dtype=jnp.int32)
    lower = order[None, :] <= order[:, None]

    def advance(state, pieces):
        x_here, b_here, c_here, d_here, r_here = pieces
        cumul = jnp.cumsum(d_here, axis=1)
        counts = jnp.cumsum(r_here)
        same = lower & (counts[:, None] == counts[None, :])
        spread = cumul[:, :, None] - cumul[:, None, :]
        weights = jnp.where(same[None], jnp.exp(jnp.minimum(spread, 0.0)), 0.0)
        scores = jnp.einsum("tgn,sgn->gts", c_here, b_here, precision=lax.Precision.HIGHEST)
        scores = jnp.repeat(scores, repeat_count, axis=0) * weights
        inner = jnp.einsum("hts,shp->thp", scores, x_here, precision=lax.Precision.HIGHEST)
        c_heads = jnp.repeat(c_here, repeat_count, axis=1)
        b_heads = jnp.repeat(b_here, repeat_count, axis=1)
        entry = jnp.exp(cumul) * (counts == 0).astype(jnp.float32)[None, :]
        carried = (
            jnp.einsum("thn,hpn->thp", c_heads, state, precision=lax.Precision.HIGHEST)
            * entry.T[:, :, None]
        )
        tail = jnp.exp(cumul[:, -1:] - cumul) * (counts == counts[-1]).astype(jnp.float32)[None, :]
        fresh = jnp.einsum(
            "shp,shn->hpn", x_here * tail.T[:, :, None], b_heads, precision=lax.Precision.HIGHEST
        )
        passing = entry[:, -1]
        return (fresh + passing[:, None, None] * state, inner + carried)

    final, outputs = lax.scan(
        jax.checkpoint(advance), start_state, (x_blocks, b_blocks, c_blocks, d_blocks, r_blocks)
    )
    return (outputs.reshape(tokens_here, heads_here * P_SIZE), final)


def gated_norm(values, gate, gain):
    gated = values * jax.nn.silu(gate)
    rows_here, width = gated.shape
    group_width = HP // G
    grouped = gated.reshape(rows_here, width // group_width, group_width)
    scale = lax.rsqrt(jnp.mean(grouped * grouped, axis=2, keepdims=True) + 1e-05)
    return (grouped * scale).reshape(rows_here, width) * gain[None, :]


def carried_term(inputs_c, log_decay, resets, state):
    heads_here = log_decay.shape[0]
    tokens_here = inputs_c.shape[0]
    groups_here = inputs_c.shape[1] // N
    cumul = jnp.cumsum(log_decay, axis=1)
    counts = jnp.cumsum(resets)
    entry = jnp.exp(cumul) * (counts == 0).astype(jnp.float32)[None, :]
    c_heads = jnp.repeat(
        inputs_c.reshape(tokens_here, groups_here, N), heads_here // groups_here, axis=1
    )
    result = (
        jnp.einsum("thn,hpn->thp", c_heads, state, precision=lax.Precision.HIGHEST)
        * entry.T[:, :, None]
    )
    return result.reshape(tokens_here, heads_here * P_SIZE)


def device_decay(log_decay, resets):
    return jnp.exp(jnp.sum(log_decay, axis=1)) * (jnp.sum(resets) == 0).astype(jnp.float32)


def per_device(
    inputs_x, inputs_b, inputs_c, gate_z, log_decay, resets, norm_gain, out_weight, out_grad
):
    x_float = inputs_x.astype(jnp.float32)
    b_float = inputs_b.astype(jnp.float32)
    c_float = inputs_c.astype(jnp.float32)
    z_float = gate_z.astype(jnp.float32)
    heads_here = log_decay.shape[0]
    zero_state = jnp.zeros((heads_here, P_SIZE, N), jnp.float32)

    def local_scan(x_arg, b_arg, c_arg, decay_arg):
        return span_scan(x_arg, b_arg, c_arg, decay_arg, resets, zero_state)

    (y_zero, s_local), pull_scan = jax.vjp(local_scan, x_float, b_float, c_float, log_decay)

    def whole_decay(decay_arg):
        return device_decay(decay_arg, resets)

    g_local, pull_decay = jax.vjp(whole_decay, log_decay)

    state_in = prefix_combine(g_local, s_local, 1)

    def finish(y_arg, c_arg, decay_arg, z_arg, state_arg):
        return gated_norm(
            y_arg + carried_term(c_arg, decay_arg, resets, state_arg), z_arg, norm_gain
        )

    normed, pull_finish = jax.vjp(finish, y_zero, c_float, log_decay, z_float, state_in)
    normed_bf = normed.astype(jnp.bfloat16)
    full_weight = lax.all_gather(out_weight, "seq", axis=0, tiled=True)
    partial_value = lax.dot_general(
        normed_bf, full_weight, (((1,), (1,)), ((), ())), preferred_element_type=jnp.float32
    )
    layer_out = lax.psum_scatter(
        partial_value.astype(jnp.bfloat16), "head", scatter_dimension=1, tiled=True
    )
    grad_full = lax.all_gather(out_grad, "head", axis=1, tiled=True)
    grad_y = jnp.dot(grad_full, full_weight, preferred_element_type=jnp.float32)
    grad_weight = lax.psum_scatter(
        lax.dot_general(
            grad_full, normed_bf, (((0,), (0,)), ((), ())), preferred_element_type=jnp.float32
        ).astype(jnp.bfloat16),
        "seq",
        scatter_dimension=0,
        tiled=True,
    ).astype(jnp.float32)
    d_zero, d_c_two, d_decay_two, grad_z, adjoint_in = pull_finish(grad_y)

    adjoint_out = prefix_combine(g_local, adjoint_in, -1)
    grad_x, grad_b, d_c_one, d_decay_one = pull_scan((d_zero, adjoint_out))
    (d_decay_three,) = pull_decay(jnp.sum(adjoint_out * state_in, axis=(1, 2)))
    return (
        layer_out,
        grad_x,
        grad_b,
        d_c_one + d_c_two,
        grad_z,
        d_decay_one + d_decay_two + d_decay_three,
        grad_weight,
    )


def solution(mesh):
    return jax.shard_map(
        per_device,
        mesh=mesh,
        in_specs=(
            P("seq", "head"),
            P("seq", "head"),
            P("seq", "head"),
            P("seq", "head"),
            P("head", "seq"),
            P("seq"),
            P("head"),
            P("seq", "head"),
            P("seq", "head"),
        ),
        out_specs=(
            P("seq", "head"),
            P("seq", "head"),
            P("seq", "head"),
            P("seq", "head"),
            P("seq", "head"),
            P("head", "seq"),
            P("seq", "head"),
        ),
        check_vma=False,
    )
```

```python
import jax
import jax.numpy as jnp
from jax import lax
from jax.sharding import PartitionSpec as P

P_SIZE = 64
N = 128
G = 8
SPAN = 256
HP = 8192


def from_behind(value, axis, steps):
    count = lax.axis_size(axis)
    leading, last = (max(0, -steps), min(count, count - steps))
    return lax.ppermute(value, axis, [(source, source + steps) for source in range(leading, last)])


def prefix_combine(decay, value, direction):
    count = lax.axis_size("seq")

    def shifted(item, steps):
        return from_behind(item, "seq", direction * steps)

    def sent(item):
        return item.astype(jnp.bfloat16)

    near = shifted(sent(value), 1).astype(jnp.float32)
    total = near
    window_decay = shifted(decay, 1)
    window = 1
    if count > 2:
        far = shifted(sent(value), 2).astype(jnp.float32)
        total = near + window_decay[:, None, None] * far
        window_decay = window_decay * shifted(decay, 2)
        window = 2
    while window < count - 1:
        incoming = shifted(sent(total), window).astype(jnp.float32)
        next_decay = None
        if 2 * window < count - 1:
            next_decay = window_decay * shifted(window_decay, window)
        total = total + window_decay[:, None, None] * incoming
        window_decay = next_decay
        window *= 2
    return total


def head_gather(block):
    count = lax.axis_size("head")
    width = block.shape[1]
    pieces = [block]
    for offset in range(1, count):
        pieces.append(
            lax.ppermute(block, "head", [((peer + offset) % count, peer) for peer in range(count)])
        )
    relative = jnp.concatenate(pieces, axis=1)
    return jnp.roll(relative, lax.axis_index("head") * width, axis=1)


def head_sum_scatter(full):
    count = lax.axis_size("head")
    width = full.shape[1] // count
    relative = jnp.roll(full, -lax.axis_index("head") * width, axis=1)
    total = relative[:, :width].astype(jnp.float32)
    for offset in range(1, count):
        piece = relative[:, offset * width:(offset + 1) * width]
        total = total + lax.ppermute(
            piece, "head", [(peer, (peer + offset) % count) for peer in range(count)]
        ).astype(jnp.float32)
    return total


def span_scan(inputs_x, inputs_b, inputs_c, log_decay, resets, start_state):
    tokens_here = inputs_x.shape[0]
    heads_here = log_decay.shape[0]
    groups_here = inputs_b.shape[1] // N
    repeat_count = heads_here // groups_here
    blocks = tokens_here // SPAN
    x_blocks = inputs_x.reshape(blocks, SPAN, heads_here, P_SIZE)
    b_blocks = inputs_b.reshape(blocks, SPAN, groups_here, N)
    c_blocks = inputs_c.reshape(blocks, SPAN, groups_here, N)
    d_blocks = log_decay.reshape(heads_here, blocks, SPAN).transpose(1, 0, 2)
    r_blocks = resets.reshape(blocks, SPAN)
    order = jnp.arange(SPAN, dtype=jnp.int32)
    lower = order[None, :] <= order[:, None]

    def advance(state, pieces):
        x_here, b_here, c_here, d_here, r_here = pieces
        cumul = jnp.cumsum(d_here, axis=1)
        counts = jnp.cumsum(r_here)
        same = lower & (counts[:, None] == counts[None, :])
        spread = cumul[:, :, None] - cumul[:, None, :]
        weights = jnp.where(same[None], jnp.exp(jnp.minimum(spread, 0.0)), 0.0)
        scores = jnp.einsum("tgn,sgn->gts", c_here, b_here, precision=lax.Precision.HIGHEST)
        scores = jnp.repeat(scores, repeat_count, axis=0) * weights
        inner = jnp.einsum("hts,shp->thp", scores, x_here, precision=lax.Precision.HIGHEST)
        c_heads = jnp.repeat(c_here, repeat_count, axis=1)
        b_heads = jnp.repeat(b_here, repeat_count, axis=1)
        entry = jnp.exp(cumul) * (counts == 0).astype(jnp.float32)[None, :]
        carried = (
            jnp.einsum("thn,hpn->thp", c_heads, state, precision=lax.Precision.HIGHEST)
            * entry.T[:, :, None]
        )
        tail = jnp.exp(cumul[:, -1:] - cumul) * (counts == counts[-1]).astype(jnp.float32)[None, :]
        fresh = jnp.einsum(
            "shp,shn->hpn", x_here * tail.T[:, :, None], b_heads, precision=lax.Precision.HIGHEST
        )
        passing = entry[:, -1]
        return (fresh + passing[:, None, None] * state, inner + carried)

    final, outputs = lax.scan(
        jax.checkpoint(advance), start_state, (x_blocks, b_blocks, c_blocks, d_blocks, r_blocks)
    )
    return (outputs.reshape(tokens_here, heads_here * P_SIZE), final)


def gated_norm(values, gate, gain):
    gated = values * jax.nn.silu(gate)
    rows_here, width = gated.shape
    group_width = HP // G
    grouped = gated.reshape(rows_here, width // group_width, group_width)
    scale = lax.rsqrt(jnp.mean(grouped * grouped, axis=2, keepdims=True) + 1e-05)
    return (grouped * scale).reshape(rows_here, width) * gain[None, :]


def carried_term(inputs_c, log_decay, resets, state):
    heads_here = log_decay.shape[0]
    tokens_here = inputs_c.shape[0]
    groups_here = inputs_c.shape[1] // N
    cumul = jnp.cumsum(log_decay, axis=1)
    counts = jnp.cumsum(resets)
    entry = jnp.exp(cumul) * (counts == 0).astype(jnp.float32)[None, :]
    c_heads = jnp.repeat(
        inputs_c.reshape(tokens_here, groups_here, N), heads_here // groups_here, axis=1
    )
    result = (
        jnp.einsum("thn,hpn->thp", c_heads, state, precision=lax.Precision.HIGHEST)
        * entry.T[:, :, None]
    )
    return result.reshape(tokens_here, heads_here * P_SIZE)


def device_decay(log_decay, resets):
    return jnp.exp(jnp.sum(log_decay, axis=1)) * (jnp.sum(resets) == 0).astype(jnp.float32)


def per_device(
    inputs_x, inputs_b, inputs_c, gate_z, log_decay, resets, norm_gain, out_weight, out_grad
):
    x_float = inputs_x.astype(jnp.float32)
    b_float = inputs_b.astype(jnp.float32)
    c_float = inputs_c.astype(jnp.float32)
    z_float = gate_z.astype(jnp.float32)
    heads_here = log_decay.shape[0]
    zero_state = jnp.zeros((heads_here, P_SIZE, N), jnp.float32)

    def local_scan(x_arg, b_arg, c_arg, decay_arg):
        return span_scan(x_arg, b_arg, c_arg, decay_arg, resets, zero_state)

    (y_zero, s_local), pull_scan = jax.vjp(local_scan, x_float, b_float, c_float, log_decay)

    def whole_decay(decay_arg):
        return device_decay(decay_arg, resets)

    g_local, pull_decay = jax.vjp(whole_decay, log_decay)

    state_in = prefix_combine(g_local, s_local, 1)

    def finish(y_arg, c_arg, decay_arg, z_arg, state_arg):
        return gated_norm(
            y_arg + carried_term(c_arg, decay_arg, resets, state_arg), z_arg, norm_gain
        )

    normed, pull_finish = jax.vjp(finish, y_zero, c_float, log_decay, z_float, state_in)
    normed_bf = normed.astype(jnp.bfloat16)
    full_weight = lax.all_gather(out_weight, "seq", axis=0, tiled=True)
    partial_value = lax.dot_general(
        normed_bf, full_weight, (((1,), (1,)), ((), ())), preferred_element_type=jnp.float32
    )
    layer_out = head_sum_scatter(partial_value.astype(jnp.bfloat16)).astype(jnp.bfloat16)
    grad_full = head_gather(out_grad)
    grad_y = jnp.dot(grad_full, full_weight, preferred_element_type=jnp.float32)
    grad_weight = lax.psum_scatter(
        lax.dot_general(
            grad_full, normed_bf, (((0,), (0,)), ((), ())), preferred_element_type=jnp.float32
        ).astype(jnp.bfloat16),
        "seq",
        scatter_dimension=0,
        tiled=True,
    ).astype(jnp.float32)
    d_zero, d_c_two, d_decay_two, grad_z, adjoint_in = pull_finish(grad_y)

    adjoint_out = prefix_combine(g_local, adjoint_in, -1)
    grad_x, grad_b, d_c_one, d_decay_one = pull_scan((d_zero, adjoint_out))
    (d_decay_three,) = pull_decay(jnp.sum(adjoint_out * state_in, axis=(1, 2)))
    return (
        layer_out,
        grad_x,
        grad_b,
        d_c_one + d_c_two,
        grad_z,
        d_decay_one + d_decay_two + d_decay_three,
        grad_weight,
    )


def solution(mesh):
    return jax.shard_map(
        per_device,
        mesh=mesh,
        in_specs=(
            P("seq", "head"),
            P("seq", "head"),
            P("seq", "head"),
            P("seq", "head"),
            P("head", "seq"),
            P("seq"),
            P("head"),
            P("seq", "head"),
            P("seq", "head"),
        ),
        out_specs=(
            P("seq", "head"),
            P("seq", "head"),
            P("seq", "head"),
            P("seq", "head"),
            P("seq", "head"),
            P("head", "seq"),
            P("seq", "head"),
        ),
        check_vma=False,
    )
```

```python
import jax
import jax.numpy as jnp
from jax import lax
from jax.sharding import PartitionSpec as P

P_SIZE = 64
N = 128
G = 8
SPAN = 256
HP = 8192


def from_behind(value, axis, steps):
    count = lax.axis_size(axis)
    leading, last = (max(0, -steps), min(count, count - steps))
    return lax.ppermute(value, axis, [(source, source + steps) for source in range(leading, last)])


def prefix_combine(decay, value, direction):
    count = lax.axis_size("seq")

    def shifted(item, steps):
        return from_behind(item, "seq", direction * steps)

    def sent(item):
        return item.astype(jnp.bfloat16)

    near = shifted(sent(value), 1).astype(jnp.float32)
    total = near
    window_decay = shifted(decay, 1)
    window = 1
    if count > 2:
        far = shifted(sent(value), 2).astype(jnp.float32)
        total = near + window_decay[:, None, None] * far
        window_decay = window_decay * shifted(decay, 2)
        window = 2
    while window < count - 1:
        incoming = shifted(sent(total), window).astype(jnp.float32)
        next_decay = None
        if 2 * window < count - 1:
            next_decay = window_decay * shifted(window_decay, window)
        total = total + window_decay[:, None, None] * incoming
        window_decay = next_decay
        window *= 2
    return total


def head_gather(block):
    count = lax.axis_size("head")
    width = block.shape[1]
    pieces = [block]
    for offset in range(1, count):
        pieces.append(
            lax.ppermute(block, "head", [((peer + offset) % count, peer) for peer in range(count)])
        )
    relative = jnp.concatenate(pieces, axis=1)
    return jnp.roll(relative, lax.axis_index("head") * width, axis=1)


def head_sum_scatter(full):
    count = lax.axis_size("head")
    width = full.shape[1] // count
    relative = jnp.roll(full, -lax.axis_index("head") * width, axis=1)
    total = relative[:, :width].astype(jnp.float32)
    for offset in range(1, count):
        piece = relative[:, offset * width:(offset + 1) * width]
        total = total + lax.ppermute(
            piece, "head", [(peer, (peer + offset) % count) for peer in range(count)]
        ).astype(jnp.float32)
    return total


def block_setup(x_arg, b_arg, decay_arg, resets):
    tokens_here = x_arg.shape[0]
    heads_here = decay_arg.shape[0]
    groups_here = b_arg.shape[1] // N
    x_heads = x_arg.reshape(tokens_here, heads_here, P_SIZE)
    b_groups = b_arg.reshape(tokens_here, groups_here, N)
    cumul = jnp.cumsum(decay_arg, axis=1)
    counts = jnp.cumsum(resets)
    return x_heads, b_groups, cumul, counts, heads_here // groups_here


def block_outputs(x_arg, b_arg, c_arg, decay_arg, resets):
    x_heads, b_groups, cumul, counts, repeat_count = block_setup(x_arg, b_arg, decay_arg, resets)
    tokens_here = x_arg.shape[0]
    c_groups = c_arg.reshape(tokens_here, b_groups.shape[1], N)
    order = jnp.arange(tokens_here, dtype=jnp.int32)
    lower = order[None, :] <= order[:, None]
    same = lower & (counts[:, None] == counts[None, :])
    spread = cumul[:, :, None] - cumul[:, None, :]
    weights = jnp.where(same[None], jnp.exp(jnp.minimum(spread, 0.0)), 0.0)
    scores = jnp.einsum("tgn,sgn->gts", c_groups, b_groups, precision=lax.Precision.HIGHEST)
    scores = jnp.repeat(scores, repeat_count, axis=0) * weights
    inner = jnp.einsum("hts,shp->thp", scores, x_heads, precision=lax.Precision.HIGHEST)
    return inner.reshape(tokens_here, -1)


def block_final(x_arg, b_arg, decay_arg, resets):
    x_heads, b_groups, cumul, counts, repeat_count = block_setup(x_arg, b_arg, decay_arg, resets)
    tail = jnp.exp(cumul[:, -1:] - cumul) * (counts == counts[-1]).astype(jnp.float32)[None, :]
    b_heads = jnp.repeat(b_groups, repeat_count, axis=1)
    return jnp.einsum(
        "shp,shn->hpn", x_heads * tail.T[:, :, None], b_heads, precision=lax.Precision.HIGHEST
    )


def gated_norm(values, gate, gain):
    gated = values * jax.nn.silu(gate)
    rows_here, width = gated.shape
    group_width = HP // G
    grouped = gated.reshape(rows_here, width // group_width, group_width)
    scale = lax.rsqrt(jnp.mean(grouped * grouped, axis=2, keepdims=True) + 1e-05)
    return (grouped * scale).reshape(rows_here, width) * gain[None, :]


def carried_term(inputs_c, log_decay, resets, state):
    heads_here = log_decay.shape[0]
    tokens_here = inputs_c.shape[0]
    groups_here = inputs_c.shape[1] // N
    cumul = jnp.cumsum(log_decay, axis=1)
    counts = jnp.cumsum(resets)
    entry = jnp.exp(cumul) * (counts == 0).astype(jnp.float32)[None, :]
    c_heads = jnp.repeat(
        inputs_c.reshape(tokens_here, groups_here, N), heads_here // groups_here, axis=1
    )
    result = (
        jnp.einsum("thn,hpn->thp", c_heads, state, precision=lax.Precision.HIGHEST)
        * entry.T[:, :, None]
    )
    return result.reshape(tokens_here, heads_here * P_SIZE)


def device_decay(log_decay, resets):
    return jnp.exp(jnp.sum(log_decay, axis=1)) * (jnp.sum(resets) == 0).astype(jnp.float32)


def per_device(
    inputs_x, inputs_b, inputs_c, gate_z, log_decay, resets, norm_gain, out_weight, out_grad
):
    x_float = inputs_x.astype(jnp.float32)
    b_float = inputs_b.astype(jnp.float32)
    c_float = inputs_c.astype(jnp.float32)
    z_float = gate_z.astype(jnp.float32)
    heads_here = log_decay.shape[0]

    assert inputs_x.shape[0] == SPAN

    def local_outputs(x_arg, b_arg, c_arg, decay_arg):
        return block_outputs(x_arg, b_arg, c_arg, decay_arg, resets)

    def local_final(x_arg, b_arg, decay_arg):
        return block_final(x_arg, b_arg, decay_arg, resets)

    y_zero, pull_outputs = jax.vjp(local_outputs, x_float, b_float, c_float, log_decay)
    s_local, pull_final = jax.vjp(local_final, x_float, b_float, log_decay)

    def whole_decay(decay_arg):
        return device_decay(decay_arg, resets)

    g_local, pull_decay = jax.vjp(whole_decay, log_decay)

    state_in = prefix_combine(g_local, s_local, 1)

    def finish(y_arg, c_arg, decay_arg, z_arg, state_arg):
        return gated_norm(
            y_arg + carried_term(c_arg, decay_arg, resets, state_arg), z_arg, norm_gain
        )

    normed, pull_finish = jax.vjp(finish, y_zero, c_float, log_decay, z_float, state_in)
    normed_bf = normed.astype(jnp.bfloat16)
    full_weight = lax.all_gather(out_weight, "seq", axis=0, tiled=True)
    partial_value = lax.dot_general(
        normed_bf, full_weight, (((1,), (1,)), ((), ())), preferred_element_type=jnp.float32
    )
    layer_out = head_sum_scatter(partial_value.astype(jnp.bfloat16)).astype(jnp.bfloat16)
    grad_full = head_gather(out_grad)
    grad_y = jnp.dot(grad_full, full_weight, preferred_element_type=jnp.float32)
    grad_weight = lax.psum_scatter(
        lax.dot_general(
            grad_full, normed_bf, (((0,), (0,)), ((), ())), preferred_element_type=jnp.float32
        ).astype(jnp.bfloat16),
        "seq",
        scatter_dimension=0,
        tiled=True,
    ).astype(jnp.float32)
    d_zero, d_c_two, d_decay_two, grad_z, adjoint_in = pull_finish(grad_y)

    adjoint_out = prefix_combine(g_local, adjoint_in, -1)
    x_one, b_one, d_c_one, decay_one = pull_outputs(d_zero)
    x_two, b_two, decay_two = pull_final(adjoint_out)
    grad_x = x_one + x_two
    grad_b = b_one + b_two
    d_decay_one = decay_one + decay_two
    (d_decay_three,) = pull_decay(jnp.sum(adjoint_out * state_in, axis=(1, 2)))
    return (
        layer_out,
        grad_x,
        grad_b,
        d_c_one + d_c_two,
        grad_z,
        d_decay_one + d_decay_two + d_decay_three,
        grad_weight,
    )


def solution(mesh):
    return jax.shard_map(
        per_device,
        mesh=mesh,
        in_specs=(
            P("seq", "head"),
            P("seq", "head"),
            P("seq", "head"),
            P("seq", "head"),
            P("head", "seq"),
            P("seq"),
            P("head"),
            P("seq", "head"),
            P("seq", "head"),
        ),
        out_specs=(
            P("seq", "head"),
            P("seq", "head"),
            P("seq", "head"),
            P("seq", "head"),
            P("seq", "head"),
            P("head", "seq"),
            P("seq", "head"),
        ),
        check_vma=False,
    )
```

```python
import jax
import jax.numpy as jnp
from jax import lax
from jax.sharding import PartitionSpec as P

P_SIZE = 64
N = 128
G = 8
SPAN = 256
HP = 8192


def from_behind(value, axis, steps):
    count = lax.axis_size(axis)
    leading, last = (max(0, -steps), min(count, count - steps))
    return lax.ppermute(value, axis, [(source, source + steps) for source in range(leading, last)])


def prefix_combine(decay_all, value, direction, width=4):
    count = lax.axis_size("seq")
    distance = (lax.axis_index("seq") - jnp.arange(count)) * direction

    def between(steps):
        inside = (distance > 0) & (distance < steps)
        return jnp.prod(jnp.where(inside[:, None], decay_all, 1.0), axis=0)[:, None, None]

    def shifted(item, steps):
        return from_behind(item.astype(jnp.bfloat16), "seq", direction * steps).astype(jnp.float32)

    near = min(width, count - 1)
    total = shifted(value, 1)
    for steps in range(2, near + 1):
        total = total + between(steps) * shifted(value, steps)
    result = total
    for steps in range(near, count - 1, near):
        result = result + between(steps + 1) * shifted(total, steps)
    return result


def head_gather(block):
    count = lax.axis_size("head")
    width = block.shape[1]
    pieces = [block]
    for offset in range(1, count):
        pieces.append(
            lax.ppermute(block, "head", [((peer + offset) % count, peer) for peer in range(count)])
        )
    relative = jnp.concatenate(pieces, axis=1)
    return jnp.roll(relative, lax.axis_index("head") * width, axis=1)


def head_sum_scatter(full):
    count = lax.axis_size("head")
    width = full.shape[1] // count
    relative = jnp.roll(full, -lax.axis_index("head") * width, axis=1)
    total = relative[:, :width].astype(jnp.float32)
    for offset in range(1, count):
        piece = relative[:, offset * width:(offset + 1) * width]
        total = total + lax.ppermute(
            piece, "head", [(peer, (peer + offset) % count) for peer in range(count)]
        ).astype(jnp.float32)
    return total


def block_setup(x_arg, b_arg, decay_arg, resets):
    tokens_here = x_arg.shape[0]
    heads_here = decay_arg.shape[0]
    groups_here = b_arg.shape[1] // N
    x_heads = x_arg.reshape(tokens_here, heads_here, P_SIZE)
    b_groups = b_arg.reshape(tokens_here, groups_here, N)
    cumul = jnp.cumsum(decay_arg, axis=1)
    counts = jnp.cumsum(resets)
    return x_heads, b_groups, cumul, counts, heads_here // groups_here


def block_outputs(x_arg, b_arg, c_arg, decay_arg, resets):
    x_heads, b_groups, cumul, counts, repeat_count = block_setup(x_arg, b_arg, decay_arg, resets)
    tokens_here = x_arg.shape[0]
    c_groups = c_arg.reshape(tokens_here, b_groups.shape[1], N)
    order = jnp.arange(tokens_here, dtype=jnp.int32)
    lower = order[None, :] <= order[:, None]
    same = lower & (counts[:, None] == counts[None, :])
    spread = cumul[:, :, None] - cumul[:, None, :]
    weights = jnp.where(same[None], jnp.exp(jnp.minimum(spread, 0.0)), 0.0)
    scores = jnp.einsum("tgn,sgn->gts", c_groups, b_groups, precision=lax.Precision.HIGHEST)
    scores = jnp.repeat(scores, repeat_count, axis=0) * weights
    inner = jnp.einsum("hts,shp->thp", scores, x_heads, precision=lax.Precision.HIGHEST)
    return inner.reshape(tokens_here, -1)


def block_final(x_arg, b_arg, decay_arg, resets):
    x_heads, b_groups, cumul, counts, repeat_count = block_setup(x_arg, b_arg, decay_arg, resets)
    tail = jnp.exp(cumul[:, -1:] - cumul) * (counts == counts[-1]).astype(jnp.float32)[None, :]
    b_heads = jnp.repeat(b_groups, repeat_count, axis=1)
    return jnp.einsum(
        "shp,shn->hpn", x_heads * tail.T[:, :, None], b_heads, precision=lax.Precision.HIGHEST
    )


def gated_norm(values, gate, gain):
    gated = values * jax.nn.silu(gate)
    rows_here, width = gated.shape
    group_width = HP // G
    grouped = gated.reshape(rows_here, width // group_width, group_width)
    scale = lax.rsqrt(jnp.mean(grouped * grouped, axis=2, keepdims=True) + 1e-05)
    return (grouped * scale).reshape(rows_here, width) * gain[None, :]


def carried_term(inputs_c, log_decay, resets, state):
    heads_here = log_decay.shape[0]
    tokens_here = inputs_c.shape[0]
    groups_here = inputs_c.shape[1] // N
    cumul = jnp.cumsum(log_decay, axis=1)
    counts = jnp.cumsum(resets)
    entry = jnp.exp(cumul) * (counts == 0).astype(jnp.float32)[None, :]
    c_heads = jnp.repeat(
        inputs_c.reshape(tokens_here, groups_here, N), heads_here // groups_here, axis=1
    )
    result = (
        jnp.einsum("thn,hpn->thp", c_heads, state, precision=lax.Precision.HIGHEST)
        * entry.T[:, :, None]
    )
    return result.reshape(tokens_here, heads_here * P_SIZE)


def device_decay(log_decay, resets):
    return jnp.exp(jnp.sum(log_decay, axis=1)) * (jnp.sum(resets) == 0).astype(jnp.float32)


def per_device(
    inputs_x, inputs_b, inputs_c, gate_z, log_decay, resets, norm_gain, out_weight, out_grad
):
    x_float = inputs_x.astype(jnp.float32)
    b_float = inputs_b.astype(jnp.float32)
    c_float = inputs_c.astype(jnp.float32)
    z_float = gate_z.astype(jnp.float32)
    heads_here = log_decay.shape[0]

    assert inputs_x.shape[0] == SPAN

    def local_outputs(x_arg, b_arg, c_arg, decay_arg):
        return block_outputs(x_arg, b_arg, c_arg, decay_arg, resets)

    def local_final(x_arg, b_arg, decay_arg):
        return block_final(x_arg, b_arg, decay_arg, resets)

    y_zero, pull_outputs = jax.vjp(local_outputs, x_float, b_float, c_float, log_decay)
    s_local, pull_final = jax.vjp(local_final, x_float, b_float, log_decay)

    def whole_decay(decay_arg):
        return device_decay(decay_arg, resets)

    g_local, pull_decay = jax.vjp(whole_decay, log_decay)

    g_all = lax.all_gather(g_local, "seq")
    state_in = prefix_combine(g_all, s_local, 1)

    def finish(y_arg, c_arg, decay_arg, z_arg, state_arg):
        return gated_norm(
            y_arg + carried_term(c_arg, decay_arg, resets, state_arg), z_arg, norm_gain
        )

    normed, pull_finish = jax.vjp(finish, y_zero, c_float, log_decay, z_float, state_in)
    normed_bf = normed.astype(jnp.bfloat16)
    full_weight = lax.all_gather(out_weight, "seq", axis=0, tiled=True)
    partial_value = lax.dot_general(
        normed_bf, full_weight, (((1,), (1,)), ((), ())), preferred_element_type=jnp.float32
    )
    layer_out = head_sum_scatter(partial_value.astype(jnp.bfloat16)).astype(jnp.bfloat16)
    grad_full = head_gather(out_grad)
    grad_y = jnp.dot(grad_full, full_weight, preferred_element_type=jnp.float32)
    seq_count = lax.axis_size("seq")
    tokens_here = normed_bf.shape[0]
    normed_all = lax.all_gather(normed_bf, "seq", axis=0, tiled=True)
    feature_rows = out_weight.shape[0]
    grad_columns = lax.all_to_all(
        grad_full.reshape(tokens_here, seq_count, feature_rows),
        "seq",
        split_axis=1,
        concat_axis=0,
        tiled=True,
    ).reshape(seq_count, tokens_here, feature_rows)
    weight_terms = jnp.einsum(
        "btf,btc->bfc",
        grad_columns,
        normed_all.reshape(seq_count, tokens_here, -1),
        preferred_element_type=jnp.float32,
    )
    grad_weight = jnp.sum(weight_terms.astype(jnp.bfloat16).astype(jnp.float32), axis=0)
    d_zero, d_c_two, d_decay_two, grad_z, adjoint_in = pull_finish(grad_y)

    adjoint_out = prefix_combine(g_all, adjoint_in, -1)
    x_one, b_one, d_c_one, decay_one = pull_outputs(d_zero)
    x_two, b_two, decay_two = pull_final(adjoint_out)
    grad_x = x_one + x_two
    grad_b = b_one + b_two
    d_decay_one = decay_one + decay_two
    (d_decay_three,) = pull_decay(jnp.sum(adjoint_out * state_in, axis=(1, 2)))
    return (
        layer_out,
        grad_x,
        grad_b,
        d_c_one + d_c_two,
        grad_z,
        d_decay_one + d_decay_two + d_decay_three,
        grad_weight,
    )


def solution(mesh):
    return jax.shard_map(
        per_device,
        mesh=mesh,
        in_specs=(
            P("seq", "head"),
            P("seq", "head"),
            P("seq", "head"),
            P("seq", "head"),
            P("head", "seq"),
            P("seq"),
            P("head"),
            P("seq", "head"),
            P("seq", "head"),
        ),
        out_specs=(
            P("seq", "head"),
            P("seq", "head"),
            P("seq", "head"),
            P("seq", "head"),
            P("seq", "head"),
            P("head", "seq"),
            P("seq", "head"),
        ),
        check_vma=False,
    )
```

```python
import jax
import jax.numpy as jnp
from jax import lax
from jax.sharding import PartitionSpec as P

P_SIZE = 64
N = 128
G = 8
SPAN = 256
HP = 8192


def from_behind(value, axis, steps):
    count = lax.axis_size(axis)
    leading, last = (max(0, -steps), min(count, count - steps))
    return lax.ppermute(value, axis, [(source, source + steps) for source in range(leading, last)])


def with_decay(state, decay):
    high = decay.astype(jnp.bfloat16)
    low = (decay - high.astype(jnp.float32)).astype(jnp.bfloat16)
    rows = jnp.zeros((state.shape[0], 8, state.shape[2]), jnp.bfloat16)
    rows = rows.at[:, 0, :].set(high[:, None]).at[:, 1, :].set(low[:, None])
    return jnp.concatenate([state.astype(jnp.bfloat16), rows], axis=1)


def split_decay(payload, rows):
    state = payload[:, :rows].astype(jnp.float32)
    decay = payload[:, rows, 0].astype(jnp.float32) + payload[:, rows + 1, 0].astype(jnp.float32)
    return state, decay


def prefix_combine(decay, value, direction, width=4):
    count = lax.axis_size("seq")
    rows = value.shape[1]

    def shifted(payload, steps):
        return split_decay(from_behind(payload, "seq", direction * steps), rows)

    near = min(width, count - 1)
    outgoing = with_decay(value, decay)
    total, passed = shifted(outgoing, 1)
    for steps in range(2, near + 1):
        item, item_decay = shifted(outgoing, steps)
        total = total + passed[:, None, None] * item
        passed = passed * item_decay
    result = total
    outgoing = with_decay(total, passed)
    through = passed
    for steps in range(near, count - 1, near):
        item, item_decay = shifted(outgoing, steps)
        result = result + through[:, None, None] * item
        through = through * item_decay
    return result


def head_gather(block):
    count = lax.axis_size("head")
    width = block.shape[1]
    pieces = [block]
    for offset in range(1, count):
        pieces.append(
            lax.ppermute(block, "head", [((peer + offset) % count, peer) for peer in range(count)])
        )
    relative = jnp.concatenate(pieces, axis=1)
    return jnp.roll(relative, lax.axis_index("head") * width, axis=1)


def head_sum_scatter(full):
    count = lax.axis_size("head")
    width = full.shape[1] // count
    relative = jnp.roll(full, -lax.axis_index("head") * width, axis=1)
    total = relative[:, :width].astype(jnp.float32)
    for offset in range(1, count):
        piece = relative[:, offset * width:(offset + 1) * width]
        total = total + lax.ppermute(
            piece, "head", [(peer, (peer + offset) % count) for peer in range(count)]
        ).astype(jnp.float32)
    return total


def block_setup(x_arg, b_arg, decay_arg, resets):
    tokens_here = x_arg.shape[0]
    heads_here = decay_arg.shape[0]
    groups_here = b_arg.shape[1] // N
    x_heads = x_arg.reshape(tokens_here, heads_here, P_SIZE)
    b_groups = b_arg.reshape(tokens_here, groups_here, N)
    cumul = jnp.cumsum(decay_arg, axis=1)
    counts = jnp.cumsum(resets)
    return x_heads, b_groups, cumul, counts, heads_here // groups_here


def block_outputs(x_arg, b_arg, c_arg, decay_arg, resets):
    x_heads, b_groups, cumul, counts, repeat_count = block_setup(x_arg, b_arg, decay_arg, resets)
    tokens_here = x_arg.shape[0]
    c_groups = c_arg.reshape(tokens_here, b_groups.shape[1], N)
    order = jnp.arange(tokens_here, dtype=jnp.int32)
    lower = order[None, :] <= order[:, None]
    same = lower & (counts[:, None] == counts[None, :])
    spread = cumul[:, :, None] - cumul[:, None, :]
    weights = jnp.where(same[None], jnp.exp(jnp.minimum(spread, 0.0)), 0.0)
    scores = jnp.einsum("tgn,sgn->gts", c_groups, b_groups, precision=lax.Precision.HIGHEST)
    scores = jnp.repeat(scores, repeat_count, axis=0) * weights
    inner = jnp.einsum("hts,shp->thp", scores, x_heads, precision=lax.Precision.HIGHEST)
    return inner.reshape(tokens_here, -1)


def block_final(x_arg, b_arg, decay_arg, resets):
    x_heads, b_groups, cumul, counts, repeat_count = block_setup(x_arg, b_arg, decay_arg, resets)
    tail = jnp.exp(cumul[:, -1:] - cumul) * (counts == counts[-1]).astype(jnp.float32)[None, :]
    b_heads = jnp.repeat(b_groups, repeat_count, axis=1)
    return jnp.einsum(
        "shp,shn->hpn", x_heads * tail.T[:, :, None], b_heads, precision=lax.Precision.HIGHEST
    )


def gated_norm(values, gate, gain):
    gated = values * jax.nn.silu(gate)
    rows_here, width = gated.shape
    group_width = HP // G
    grouped = gated.reshape(rows_here, width // group_width, group_width)
    scale = lax.rsqrt(jnp.mean(grouped * grouped, axis=2, keepdims=True) + 1e-05)
    return (grouped * scale).reshape(rows_here, width) * gain[None, :]


def carried_term(inputs_c, log_decay, resets, state):
    heads_here = log_decay.shape[0]
    tokens_here = inputs_c.shape[0]
    groups_here = inputs_c.shape[1] // N
    cumul = jnp.cumsum(log_decay, axis=1)
    counts = jnp.cumsum(resets)
    entry = jnp.exp(cumul) * (counts == 0).astype(jnp.float32)[None, :]
    c_heads = jnp.repeat(
        inputs_c.reshape(tokens_here, groups_here, N), heads_here // groups_here, axis=1
    )
    result = (
        jnp.einsum("thn,hpn->thp", c_heads, state, precision=lax.Precision.HIGHEST)
        * entry.T[:, :, None]
    )
    return result.reshape(tokens_here, heads_here * P_SIZE)


def device_decay(log_decay, resets):
    return jnp.exp(jnp.sum(log_decay, axis=1)) * (jnp.sum(resets) == 0).astype(jnp.float32)


def per_device(
    inputs_x, inputs_b, inputs_c, gate_z, log_decay, resets, norm_gain, out_weight, out_grad
):
    x_float = inputs_x.astype(jnp.float32)
    b_float = inputs_b.astype(jnp.float32)
    c_float = inputs_c.astype(jnp.float32)
    z_float = gate_z.astype(jnp.float32)
    heads_here = log_decay.shape[0]

    assert inputs_x.shape[0] == SPAN

    def local_outputs(x_arg, b_arg, c_arg, decay_arg):
        return block_outputs(x_arg, b_arg, c_arg, decay_arg, resets)

    def local_final(x_arg, b_arg, decay_arg):
        return block_final(x_arg, b_arg, decay_arg, resets)

    y_zero, pull_outputs = jax.vjp(local_outputs, x_float, b_float, c_float, log_decay)
    s_local, pull_final = jax.vjp(local_final, x_float, b_float, log_decay)

    def whole_decay(decay_arg):
        return device_decay(decay_arg, resets)

    g_local, pull_decay = jax.vjp(whole_decay, log_decay)

    state_in = prefix_combine(g_local, s_local, 1)

    def finish(y_arg, c_arg, decay_arg, z_arg, state_arg):
        return gated_norm(
            y_arg + carried_term(c_arg, decay_arg, resets, state_arg), z_arg, norm_gain
        )

    normed, pull_finish = jax.vjp(finish, y_zero, c_float, log_decay, z_float, state_in)
    normed_bf = normed.astype(jnp.bfloat16)
    full_weight = lax.all_gather(out_weight, "seq", axis=0, tiled=True)
    partial_value = lax.dot_general(
        normed_bf, full_weight, (((1,), (1,)), ((), ())), preferred_element_type=jnp.float32
    )
    layer_out = head_sum_scatter(partial_value.astype(jnp.bfloat16)).astype(jnp.bfloat16)
    grad_full = head_gather(out_grad)
    grad_y = jnp.dot(grad_full, full_weight, preferred_element_type=jnp.float32)
    grad_weight = lax.psum_scatter(
        lax.dot_general(
            grad_full, normed_bf, (((0,), (0,)), ((), ())), preferred_element_type=jnp.float32
        ).astype(jnp.bfloat16),
        "seq",
        scatter_dimension=0,
        tiled=True,
    ).astype(jnp.float32)
    d_zero, d_c_two, d_decay_two, grad_z, adjoint_in = pull_finish(grad_y)

    adjoint_out = prefix_combine(g_local, adjoint_in, -1)
    x_one, b_one, d_c_one, decay_one = pull_outputs(d_zero)
    x_two, b_two, decay_two = pull_final(adjoint_out)
    grad_x = x_one + x_two
    grad_b = b_one + b_two
    d_decay_one = decay_one + decay_two
    (d_decay_three,) = pull_decay(jnp.sum(adjoint_out * state_in, axis=(1, 2)))
    return (
        layer_out,
        grad_x,
        grad_b,
        d_c_one + d_c_two,
        grad_z,
        d_decay_one + d_decay_two + d_decay_three,
        grad_weight,
    )


def solution(mesh):
    return jax.shard_map(
        per_device,
        mesh=mesh,
        in_specs=(
            P("seq", "head"),
            P("seq", "head"),
            P("seq", "head"),
            P("seq", "head"),
            P("head", "seq"),
            P("seq"),
            P("head"),
            P("seq", "head"),
            P("seq", "head"),
        ),
        out_specs=(
            P("seq", "head"),
            P("seq", "head"),
            P("seq", "head"),
            P("seq", "head"),
            P("seq", "head"),
            P("head", "seq"),
            P("seq", "head"),
        ),
        check_vma=False,
    )
```

```python
import jax
import jax.numpy as jnp
from jax import lax
from jax.sharding import PartitionSpec as P

P_SIZE = 64
N = 128
G = 8
SPAN = 256
HP = 8192


def from_behind(value, axis, steps):
    count = lax.axis_size(axis)
    leading, last = (max(0, -steps), min(count, count - steps))
    return lax.ppermute(value, axis, [(source, source + steps) for source in range(leading, last)])


def prefix_combine(decay, value, direction):
    count = lax.axis_size("seq")

    def shifted(item, steps):
        return from_behind(item, "seq", direction * steps)

    def sent(item):
        return item.astype(jnp.bfloat16)

    near = shifted(sent(value), 1).astype(jnp.float32)
    total = near
    window_decay = shifted(decay, 1)
    window = 1
    if count > 2:
        far = shifted(sent(value), 2).astype(jnp.float32)
        total = near + window_decay[:, None, None] * far
        window_decay = window_decay * shifted(decay, 2)
        window = 2
    while window < count - 1:
        incoming = shifted(sent(total), window).astype(jnp.float32)
        next_decay = None
        if 2 * window < count - 1:
            next_decay = window_decay * shifted(window_decay, window)
        total = total + window_decay[:, None, None] * incoming
        window_decay = next_decay
        window *= 2
    return total


def head_gather(block):
    count = lax.axis_size("head")
    rows, width = block.shape
    copies = jnp.broadcast_to(block[:, None, :], (rows, count, width))
    gathered = lax.all_to_all(copies, "head", split_axis=1, concat_axis=1, tiled=True)
    return gathered.reshape(rows, count * width)


def head_sum_scatter(full):
    count = lax.axis_size("head")
    rows = full.shape[0]
    pieces = full.reshape(rows, count, -1)
    received = lax.all_to_all(pieces, "head", split_axis=1, concat_axis=1, tiled=True)
    return jnp.sum(received.astype(jnp.float32), axis=1)


def block_setup(x_arg, b_arg, decay_arg, resets):
    tokens_here = x_arg.shape[0]
    heads_here = decay_arg.shape[0]
    groups_here = b_arg.shape[1] // N
    x_heads = x_arg.reshape(tokens_here, heads_here, P_SIZE)
    b_groups = b_arg.reshape(tokens_here, groups_here, N)
    cumul = jnp.cumsum(decay_arg, axis=1)
    counts = jnp.cumsum(resets)
    return x_heads, b_groups, cumul, counts, heads_here // groups_here


def block_outputs(x_arg, b_arg, c_arg, decay_arg, resets):
    x_heads, b_groups, cumul, counts, repeat_count = block_setup(x_arg, b_arg, decay_arg, resets)
    tokens_here = x_arg.shape[0]
    c_groups = c_arg.reshape(tokens_here, b_groups.shape[1], N)
    order = jnp.arange(tokens_here, dtype=jnp.int32)
    lower = order[None, :] <= order[:, None]
    same = lower & (counts[:, None] == counts[None, :])
    spread = cumul[:, :, None] - cumul[:, None, :]
    weights = jnp.where(same[None], jnp.exp(jnp.minimum(spread, 0.0)), 0.0)
    scores = jnp.einsum("tgn,sgn->gts", c_groups, b_groups, precision=lax.Precision.HIGHEST)
    scores = jnp.repeat(scores, repeat_count, axis=0) * weights
    inner = jnp.einsum("hts,shp->thp", scores, x_heads, precision=lax.Precision.HIGHEST)
    return inner.reshape(tokens_here, -1)


def block_final(x_arg, b_arg, decay_arg, resets):
    x_heads, b_groups, cumul, counts, repeat_count = block_setup(x_arg, b_arg, decay_arg, resets)
    tail = jnp.exp(cumul[:, -1:] - cumul) * (counts == counts[-1]).astype(jnp.float32)[None, :]
    b_heads = jnp.repeat(b_groups, repeat_count, axis=1)
    return jnp.einsum(
        "shp,shn->hpn", x_heads * tail.T[:, :, None], b_heads, precision=lax.Precision.HIGHEST
    )


def gated_norm(values, gate, gain):
    gated = values * jax.nn.silu(gate)
    rows_here, width = gated.shape
    group_width = HP // G
    grouped = gated.reshape(rows_here, width // group_width, group_width)
    scale = lax.rsqrt(jnp.mean(grouped * grouped, axis=2, keepdims=True) + 1e-05)
    return (grouped * scale).reshape(rows_here, width) * gain[None, :]


def carried_term(inputs_c, log_decay, resets, state):
    heads_here = log_decay.shape[0]
    tokens_here = inputs_c.shape[0]
    groups_here = inputs_c.shape[1] // N
    cumul = jnp.cumsum(log_decay, axis=1)
    counts = jnp.cumsum(resets)
    entry = jnp.exp(cumul) * (counts == 0).astype(jnp.float32)[None, :]
    c_heads = jnp.repeat(
        inputs_c.reshape(tokens_here, groups_here, N), heads_here // groups_here, axis=1
    )
    result = (
        jnp.einsum("thn,hpn->thp", c_heads, state, precision=lax.Precision.HIGHEST)
        * entry.T[:, :, None]
    )
    return result.reshape(tokens_here, heads_here * P_SIZE)


def device_decay(log_decay, resets):
    return jnp.exp(jnp.sum(log_decay, axis=1)) * (jnp.sum(resets) == 0).astype(jnp.float32)


def per_device(
    inputs_x, inputs_b, inputs_c, gate_z, log_decay, resets, norm_gain, out_weight, out_grad
):
    x_float = inputs_x.astype(jnp.float32)
    b_float = inputs_b.astype(jnp.float32)
    c_float = inputs_c.astype(jnp.float32)
    z_float = gate_z.astype(jnp.float32)
    heads_here = log_decay.shape[0]

    assert inputs_x.shape[0] == SPAN

    def local_outputs(x_arg, b_arg, c_arg, decay_arg):
        return block_outputs(x_arg, b_arg, c_arg, decay_arg, resets)

    def local_final(x_arg, b_arg, decay_arg):
        return block_final(x_arg, b_arg, decay_arg, resets)

    y_zero, pull_outputs = jax.vjp(local_outputs, x_float, b_float, c_float, log_decay)
    s_local, pull_final = jax.vjp(local_final, x_float, b_float, log_decay)

    def whole_decay(decay_arg):
        return device_decay(decay_arg, resets)

    g_local, pull_decay = jax.vjp(whole_decay, log_decay)

    state_in = prefix_combine(g_local, s_local, 1)

    def finish(y_arg, c_arg, decay_arg, z_arg, state_arg):
        return gated_norm(
            y_arg + carried_term(c_arg, decay_arg, resets, state_arg), z_arg, norm_gain
        )

    normed, pull_finish = jax.vjp(finish, y_zero, c_float, log_decay, z_float, state_in)
    normed_bf = normed.astype(jnp.bfloat16)
    full_weight = lax.all_gather(out_weight, "seq", axis=0, tiled=True)
    partial_value = lax.dot_general(
        normed_bf, full_weight, (((1,), (1,)), ((), ())), preferred_element_type=jnp.float32
    )
    layer_out = head_sum_scatter(partial_value.astype(jnp.bfloat16)).astype(jnp.bfloat16)
    grad_full = head_gather(out_grad)
    grad_y = jnp.dot(grad_full, full_weight, preferred_element_type=jnp.float32)
    grad_weight = lax.psum_scatter(
        lax.dot_general(
            grad_full, normed_bf, (((0,), (0,)), ((), ())), preferred_element_type=jnp.float32
        ).astype(jnp.bfloat16),
        "seq",
        scatter_dimension=0,
        tiled=True,
    ).astype(jnp.float32)
    d_zero, d_c_two, d_decay_two, grad_z, adjoint_in = pull_finish(grad_y)

    adjoint_out = prefix_combine(g_local, adjoint_in, -1)
    x_one, b_one, d_c_one, decay_one = pull_outputs(d_zero)
    x_two, b_two, decay_two = pull_final(adjoint_out)
    grad_x = x_one + x_two
    grad_b = b_one + b_two
    d_decay_one = decay_one + decay_two
    (d_decay_three,) = pull_decay(jnp.sum(adjoint_out * state_in, axis=(1, 2)))
    return (
        layer_out,
        grad_x,
        grad_b,
        d_c_one + d_c_two,
        grad_z,
        d_decay_one + d_decay_two + d_decay_three,
        grad_weight,
    )


def solution(mesh):
    return jax.shard_map(
        per_device,
        mesh=mesh,
        in_specs=(
            P("seq", "head"),
            P("seq", "head"),
            P("seq", "head"),
            P("seq", "head"),
            P("head", "seq"),
            P("seq"),
            P("head"),
            P("seq", "head"),
            P("seq", "head"),
        ),
        out_specs=(
            P("seq", "head"),
            P("seq", "head"),
            P("seq", "head"),
            P("seq", "head"),
            P("seq", "head"),
            P("head", "seq"),
            P("seq", "head"),
        ),
        check_vma=False,
    )
```

```python
import jax
import jax.numpy as jnp
from jax import lax
from jax.sharding import PartitionSpec as P

P_SIZE = 64
N = 128
G = 8
SPAN = 256
HP = 8192


def from_behind(value, axis, steps):
    count = lax.axis_size(axis)
    leading, last = (max(0, -steps), min(count, count - steps))
    return lax.ppermute(value, axis, [(source, source + steps) for source in range(leading, last)])


def with_decay(state, decay):
    high = decay.astype(jnp.bfloat16)
    low = (decay - high.astype(jnp.float32)).astype(jnp.bfloat16)
    rows = jnp.zeros((state.shape[0], 8, state.shape[2]), jnp.bfloat16)
    rows = rows.at[:, 0, :].set(high[:, None]).at[:, 1, :].set(low[:, None])
    return jnp.concatenate([state.astype(jnp.bfloat16), rows], axis=1)


def split_decay(payload, rows):
    state = payload[:, :rows].astype(jnp.float32)
    decay = payload[:, rows, 0].astype(jnp.float32) + payload[:, rows + 1, 0].astype(jnp.float32)
    return state, decay


def prefix_combine(decay, value, direction, width=4):
    count = lax.axis_size("seq")
    rows = value.shape[1]

    def shifted(payload, steps):
        return split_decay(from_behind(payload, "seq", direction * steps), rows)

    near = min(width, count - 1)
    outgoing = with_decay(value, decay)
    total, passed = shifted(outgoing, 1)
    for steps in range(2, near + 1):
        item, item_decay = shifted(outgoing, steps)
        total = total + passed[:, None, None] * item
        passed = passed * item_decay
    result = total
    outgoing = with_decay(total, passed)
    through = passed
    for steps in range(near, count - 1, near):
        item, item_decay = shifted(outgoing, steps)
        result = result + through[:, None, None] * item
        through = through * item_decay
    return result


def head_gather(block):
    count = lax.axis_size("head")
    rows, width = block.shape
    copies = jnp.broadcast_to(block[:, None, :], (rows, count, width))
    gathered = lax.all_to_all(copies, "head", split_axis=1, concat_axis=1, tiled=True)
    return gathered.reshape(rows, count * width)


def head_sum_scatter(full):
    count = lax.axis_size("head")
    rows = full.shape[0]
    pieces = full.reshape(rows, count, -1)
    received = lax.all_to_all(pieces, "head", split_axis=1, concat_axis=1, tiled=True)
    return jnp.sum(received.astype(jnp.float32), axis=1)


def block_setup(x_arg, b_arg, decay_arg, resets):
    tokens_here = x_arg.shape[0]
    heads_here = decay_arg.shape[0]
    groups_here = b_arg.shape[1] // N
    x_heads = x_arg.reshape(tokens_here, heads_here, P_SIZE)
    b_groups = b_arg.reshape(tokens_here, groups_here, N)
    cumul = jnp.cumsum(decay_arg, axis=1)
    counts = jnp.cumsum(resets)
    return x_heads, b_groups, cumul, counts, heads_here // groups_here


def block_outputs(x_arg, b_arg, c_arg, decay_arg, resets):
    x_heads, b_groups, cumul, counts, repeat_count = block_setup(x_arg, b_arg, decay_arg, resets)
    tokens_here = x_arg.shape[0]
    c_groups = c_arg.reshape(tokens_here, b_groups.shape[1], N)
    order = jnp.arange(tokens_here, dtype=jnp.int32)
    lower = order[None, :] <= order[:, None]
    same = lower & (counts[:, None] == counts[None, :])
    spread = cumul[:, :, None] - cumul[:, None, :]
    weights = jnp.where(same[None], jnp.exp(jnp.minimum(spread, 0.0)), 0.0)
    scores = jnp.einsum("tgn,sgn->gts", c_groups, b_groups, precision=lax.Precision.HIGHEST)
    scores = jnp.repeat(scores, repeat_count, axis=0) * weights
    inner = jnp.einsum("hts,shp->thp", scores, x_heads, precision=lax.Precision.HIGHEST)
    return inner.reshape(tokens_here, -1)


def block_final(x_arg, b_arg, decay_arg, resets):
    x_heads, b_groups, cumul, counts, repeat_count = block_setup(x_arg, b_arg, decay_arg, resets)
    tail = jnp.exp(cumul[:, -1:] - cumul) * (counts == counts[-1]).astype(jnp.float32)[None, :]
    b_heads = jnp.repeat(b_groups, repeat_count, axis=1)
    return jnp.einsum(
        "shp,shn->hpn", x_heads * tail.T[:, :, None], b_heads, precision=lax.Precision.HIGHEST
    )


def gated_norm(values, gate, gain):
    gated = values * jax.nn.silu(gate)
    rows_here, width = gated.shape
    group_width = HP // G
    grouped = gated.reshape(rows_here, width // group_width, group_width)
    scale = lax.rsqrt(jnp.mean(grouped * grouped, axis=2, keepdims=True) + 1e-05)
    return (grouped * scale).reshape(rows_here, width) * gain[None, :]


def carried_term(inputs_c, log_decay, resets, state):
    heads_here = log_decay.shape[0]
    tokens_here = inputs_c.shape[0]
    groups_here = inputs_c.shape[1] // N
    cumul = jnp.cumsum(log_decay, axis=1)
    counts = jnp.cumsum(resets)
    entry = jnp.exp(cumul) * (counts == 0).astype(jnp.float32)[None, :]
    c_heads = jnp.repeat(
        inputs_c.reshape(tokens_here, groups_here, N), heads_here // groups_here, axis=1
    )
    result = (
        jnp.einsum("thn,hpn->thp", c_heads, state, precision=lax.Precision.HIGHEST)
        * entry.T[:, :, None]
    )
    return result.reshape(tokens_here, heads_here * P_SIZE)


def device_decay(log_decay, resets):
    return jnp.exp(jnp.sum(log_decay, axis=1)) * (jnp.sum(resets) == 0).astype(jnp.float32)


def per_device(
    inputs_x, inputs_b, inputs_c, gate_z, log_decay, resets, norm_gain, out_weight, out_grad
):
    x_float = inputs_x.astype(jnp.float32)
    b_float = inputs_b.astype(jnp.float32)
    c_float = inputs_c.astype(jnp.float32)
    z_float = gate_z.astype(jnp.float32)
    heads_here = log_decay.shape[0]

    assert inputs_x.shape[0] == SPAN

    def local_outputs(x_arg, b_arg, c_arg, decay_arg):
        return block_outputs(x_arg, b_arg, c_arg, decay_arg, resets)

    def local_final(x_arg, b_arg, decay_arg):
        return block_final(x_arg, b_arg, decay_arg, resets)

    y_zero, pull_outputs = jax.vjp(local_outputs, x_float, b_float, c_float, log_decay)
    s_local, pull_final = jax.vjp(local_final, x_float, b_float, log_decay)

    def whole_decay(decay_arg):
        return device_decay(decay_arg, resets)

    g_local, pull_decay = jax.vjp(whole_decay, log_decay)

    state_in = prefix_combine(g_local, s_local, 1)

    def finish(y_arg, c_arg, decay_arg, z_arg, state_arg):
        return gated_norm(
            y_arg + carried_term(c_arg, decay_arg, resets, state_arg), z_arg, norm_gain
        )

    normed, pull_finish = jax.vjp(finish, y_zero, c_float, log_decay, z_float, state_in)
    normed_bf = normed.astype(jnp.bfloat16)
    full_weight = lax.all_gather(out_weight, "seq", axis=0, tiled=True)
    partial_value = lax.dot_general(
        normed_bf, full_weight, (((1,), (1,)), ((), ())), preferred_element_type=jnp.float32
    )
    layer_out = head_sum_scatter(partial_value.astype(jnp.bfloat16)).astype(jnp.bfloat16)
    grad_full = head_gather(out_grad)
    grad_y = jnp.dot(grad_full, full_weight, preferred_element_type=jnp.float32)
    grad_weight = lax.psum_scatter(
        lax.dot_general(
            grad_full, normed_bf, (((0,), (0,)), ((), ())), preferred_element_type=jnp.float32
        ).astype(jnp.bfloat16),
        "seq",
        scatter_dimension=0,
        tiled=True,
    ).astype(jnp.float32)
    d_zero, d_c_two, d_decay_two, grad_z, adjoint_in = pull_finish(grad_y)

    adjoint_out = prefix_combine(g_local, adjoint_in, -1)
    x_one, b_one, d_c_one, decay_one = pull_outputs(d_zero)
    x_two, b_two, decay_two = pull_final(adjoint_out)
    grad_x = x_one + x_two
    grad_b = b_one + b_two
    d_decay_one = decay_one + decay_two
    (d_decay_three,) = pull_decay(jnp.sum(adjoint_out * state_in, axis=(1, 2)))
    return (
        layer_out,
        grad_x,
        grad_b,
        d_c_one + d_c_two,
        grad_z,
        d_decay_one + d_decay_two + d_decay_three,
        grad_weight,
    )


def solution(mesh):
    return jax.shard_map(
        per_device,
        mesh=mesh,
        in_specs=(
            P("seq", "head"),
            P("seq", "head"),
            P("seq", "head"),
            P("seq", "head"),
            P("head", "seq"),
            P("seq"),
            P("head"),
            P("seq", "head"),
            P("seq", "head"),
        ),
        out_specs=(
            P("seq", "head"),
            P("seq", "head"),
            P("seq", "head"),
            P("seq", "head"),
            P("seq", "head"),
            P("head", "seq"),
            P("seq", "head"),
        ),
        check_vma=False,
    )
```

```python
import jax
import jax.numpy as jnp
from jax import lax
from jax.sharding import PartitionSpec as P

P_SIZE = 64
N = 128
G = 8
SPAN = 256
HP = 8192


def from_behind(value, axis, steps):
    count = lax.axis_size(axis)
    leading, last = (max(0, -steps), min(count, count - steps))
    return lax.ppermute(value, axis, [(source, source + steps) for source in range(leading, last)])


def with_decay(state, decay):
    high = decay.astype(jnp.bfloat16)
    low = (decay - high.astype(jnp.float32)).astype(jnp.bfloat16)
    rows = jnp.zeros((state.shape[0], 8, state.shape[2]), jnp.bfloat16)
    rows = rows.at[:, 0, :].set(high[:, None]).at[:, 1, :].set(low[:, None])
    return jnp.concatenate([state.astype(jnp.bfloat16), rows], axis=1)


def split_decay(payload, rows):
    state = payload[:, :rows].astype(jnp.float32)
    decay = payload[:, rows, 0].astype(jnp.float32) + payload[:, rows + 1, 0].astype(jnp.float32)
    return state, decay


def prefix_combine(decay, value, direction, width=4):
    count = lax.axis_size("seq")
    rows = value.shape[1]

    def shifted(payload, steps):
        return split_decay(from_behind(payload, "seq", direction * steps), rows)

    near = min(width, count - 1)
    outgoing = with_decay(value, decay)
    total, passed = shifted(outgoing, 1)
    for steps in range(2, near + 1):
        item, item_decay = shifted(outgoing, steps)
        total = total + passed[:, None, None] * item
        passed = passed * item_decay
    result = total
    outgoing = with_decay(total, passed)
    through = passed
    for steps in range(near, count - 1, near):
        item, item_decay = shifted(outgoing, steps)
        result = result + through[:, None, None] * item
        through = through * item_decay
    return result


def head_gather(block):
    count = lax.axis_size("head")
    rows, width = block.shape
    copies = jnp.broadcast_to(block[:, None, :], (rows, count, width))
    gathered = lax.all_to_all(copies, "head", split_axis=1, concat_axis=1, tiled=True)
    return gathered.reshape(rows, count * width)


def head_sum_scatter(full):
    count = lax.axis_size("head")
    rows = full.shape[0]
    pieces = full.reshape(rows, count, -1)
    received = lax.all_to_all(pieces, "head", split_axis=1, concat_axis=1, tiled=True)
    return jnp.sum(received.astype(jnp.float32), axis=1)


def block_setup(x_arg, b_arg, decay_arg, resets):
    tokens_here = x_arg.shape[0]
    heads_here = decay_arg.shape[0]
    groups_here = b_arg.shape[1] // N
    x_heads = x_arg.reshape(tokens_here, heads_here, P_SIZE)
    b_groups = b_arg.reshape(tokens_here, groups_here, N)
    cumul = jnp.cumsum(decay_arg, axis=1)
    counts = jnp.cumsum(resets)
    return x_heads, b_groups, cumul, counts, heads_here // groups_here


def block_outputs(x_arg, b_arg, c_arg, decay_arg, resets):
    x_heads, b_groups, cumul, counts, repeat_count = block_setup(x_arg, b_arg, decay_arg, resets)
    tokens_here = x_arg.shape[0]
    c_groups = c_arg.reshape(tokens_here, b_groups.shape[1], N)
    order = jnp.arange(tokens_here, dtype=jnp.int32)
    lower = order[None, :] <= order[:, None]
    same = lower & (counts[:, None] == counts[None, :])
    spread = cumul[:, :, None] - cumul[:, None, :]
    weights = jnp.where(same[None], jnp.exp(jnp.minimum(spread, 0.0)), 0.0)
    scores = jnp.einsum("tgn,sgn->gts", c_groups, b_groups, precision=lax.Precision.HIGH)
    scores = jnp.repeat(scores, repeat_count, axis=0) * weights
    inner = jnp.einsum("hts,shp->thp", scores, x_heads, precision=lax.Precision.HIGH)
    return inner.reshape(tokens_here, -1)


def block_final(x_arg, b_arg, decay_arg, resets):
    x_heads, b_groups, cumul, counts, repeat_count = block_setup(x_arg, b_arg, decay_arg, resets)
    tail = jnp.exp(cumul[:, -1:] - cumul) * (counts == counts[-1]).astype(jnp.float32)[None, :]
    b_heads = jnp.repeat(b_groups, repeat_count, axis=1)
    return jnp.einsum(
        "shp,shn->hpn", x_heads * tail.T[:, :, None], b_heads, precision=lax.Precision.HIGH
    )


def gated_norm(values, gate, gain):
    gated = values * jax.nn.silu(gate)
    rows_here, width = gated.shape
    group_width = HP // G
    grouped = gated.reshape(rows_here, width // group_width, group_width)
    scale = lax.rsqrt(jnp.mean(grouped * grouped, axis=2, keepdims=True) + 1e-05)
    return (grouped * scale).reshape(rows_here, width) * gain[None, :]


def carried_term(inputs_c, log_decay, resets, state):
    heads_here = log_decay.shape[0]
    tokens_here = inputs_c.shape[0]
    groups_here = inputs_c.shape[1] // N
    cumul = jnp.cumsum(log_decay, axis=1)
    counts = jnp.cumsum(resets)
    entry = jnp.exp(cumul) * (counts == 0).astype(jnp.float32)[None, :]
    c_heads = jnp.repeat(
        inputs_c.reshape(tokens_here, groups_here, N), heads_here // groups_here, axis=1
    )
    result = (
        jnp.einsum("thn,hpn->thp", c_heads, state, precision=lax.Precision.HIGH)
        * entry.T[:, :, None]
    )
    return result.reshape(tokens_here, heads_here * P_SIZE)


def device_decay(log_decay, resets):
    return jnp.exp(jnp.sum(log_decay, axis=1)) * (jnp.sum(resets) == 0).astype(jnp.float32)


def per_device(
    inputs_x, inputs_b, inputs_c, gate_z, log_decay, resets, norm_gain, out_weight, out_grad
):
    x_float = inputs_x.astype(jnp.float32)
    b_float = inputs_b.astype(jnp.float32)
    c_float = inputs_c.astype(jnp.float32)
    z_float = gate_z.astype(jnp.float32)
    heads_here = log_decay.shape[0]

    assert inputs_x.shape[0] == SPAN

    def local_outputs(x_arg, b_arg, c_arg, decay_arg):
        return block_outputs(x_arg, b_arg, c_arg, decay_arg, resets)

    def local_final(x_arg, b_arg, decay_arg):
        return block_final(x_arg, b_arg, decay_arg, resets)

    y_zero, pull_outputs = jax.vjp(local_outputs, x_float, b_float, c_float, log_decay)
    s_local, pull_final = jax.vjp(local_final, x_float, b_float, log_decay)

    def whole_decay(decay_arg):
        return device_decay(decay_arg, resets)

    g_local, pull_decay = jax.vjp(whole_decay, log_decay)

    state_in = prefix_combine(g_local, s_local, 1)

    def finish(y_arg, c_arg, decay_arg, z_arg, state_arg):
        return gated_norm(
            y_arg + carried_term(c_arg, decay_arg, resets, state_arg), z_arg, norm_gain
        )

    normed, pull_finish = jax.vjp(finish, y_zero, c_float, log_decay, z_float, state_in)
    normed_bf = normed.astype(jnp.bfloat16)
    full_weight = lax.all_gather(out_weight, "seq", axis=0, tiled=True)
    partial_value = lax.dot_general(
        normed_bf, full_weight, (((1,), (1,)), ((), ())), preferred_element_type=jnp.float32
    )
    layer_out = head_sum_scatter(partial_value.astype(jnp.bfloat16)).astype(jnp.bfloat16)
    grad_full = head_gather(out_grad)
    grad_y = jnp.dot(grad_full, full_weight, preferred_element_type=jnp.float32)
    grad_weight = lax.psum_scatter(
        lax.dot_general(
            grad_full, normed_bf, (((0,), (0,)), ((), ())), preferred_element_type=jnp.float32
        ).astype(jnp.bfloat16),
        "seq",
        scatter_dimension=0,
        tiled=True,
    ).astype(jnp.float32)
    d_zero, d_c_two, d_decay_two, grad_z, adjoint_in = pull_finish(grad_y)

    adjoint_out = prefix_combine(g_local, adjoint_in, -1)
    x_one, b_one, d_c_one, decay_one = pull_outputs(d_zero)
    x_two, b_two, decay_two = pull_final(adjoint_out)
    grad_x = x_one + x_two
    grad_b = b_one + b_two
    d_decay_one = decay_one + decay_two
    (d_decay_three,) = pull_decay(jnp.sum(adjoint_out * state_in, axis=(1, 2)))
    return (
        layer_out,
        grad_x,
        grad_b,
        d_c_one + d_c_two,
        grad_z,
        d_decay_one + d_decay_two + d_decay_three,
        grad_weight,
    )


def solution(mesh):
    return jax.shard_map(
        per_device,
        mesh=mesh,
        in_specs=(
            P("seq", "head"),
            P("seq", "head"),
            P("seq", "head"),
            P("seq", "head"),
            P("head", "seq"),
            P("seq"),
            P("head"),
            P("seq", "head"),
            P("seq", "head"),
        ),
        out_specs=(
            P("seq", "head"),
            P("seq", "head"),
            P("seq", "head"),
            P("seq", "head"),
            P("seq", "head"),
            P("head", "seq"),
            P("seq", "head"),
        ),
        check_vma=False,
    )
```

```python
import jax
import jax.numpy as jnp
from jax import lax
from jax.sharding import PartitionSpec as P

P_SIZE = 64
N = 128
G = 8
SPAN = 256
HP = 8192


def from_behind(value, axis, steps):
    count = lax.axis_size(axis)
    leading, last = (max(0, -steps), min(count, count - steps))
    return lax.ppermute(value, axis, [(source, source + steps) for source in range(leading, last)])


def with_decay(state, decay):
    high = decay.astype(jnp.bfloat16)
    low = (decay - high.astype(jnp.float32)).astype(jnp.bfloat16)
    rows = jnp.zeros((state.shape[0], 8, state.shape[2]), jnp.bfloat16)
    rows = rows.at[:, 0, :].set(high[:, None]).at[:, 1, :].set(low[:, None])
    return jnp.concatenate([state.astype(jnp.bfloat16), rows], axis=1)


def split_decay(payload, rows):
    state = payload[:, :rows].astype(jnp.float32)
    decay = payload[:, rows, 0].astype(jnp.float32) + payload[:, rows + 1, 0].astype(jnp.float32)
    return state, decay


def prefix_combine(decay, value, direction, width=4):
    count = lax.axis_size("seq")
    rows = value.shape[1]

    def shifted(payload, steps):
        return split_decay(from_behind(payload, "seq", direction * steps), rows)

    near = min(width, count - 1)
    outgoing = with_decay(value, decay)
    total, passed = shifted(outgoing, 1)
    for steps in range(2, near + 1):
        item, item_decay = shifted(outgoing, steps)
        total = total + passed[:, None, None] * item
        passed = passed * item_decay
    result = total
    outgoing = with_decay(total, passed)
    through = passed
    for steps in range(near, count - 1, near):
        item, item_decay = shifted(outgoing, steps)
        result = result + through[:, None, None] * item
        through = through * item_decay
    return result


def head_gather(block):
    count = lax.axis_size("head")
    rows, width = block.shape
    copies = jnp.broadcast_to(block[:, None, :], (rows, count, width))
    gathered = lax.all_to_all(copies, "head", split_axis=1, concat_axis=1, tiled=True)
    return gathered.reshape(rows, count * width)


def head_sum_scatter(full):
    count = lax.axis_size("head")
    rows = full.shape[0]
    pieces = full.reshape(rows, count, -1)
    received = lax.all_to_all(pieces, "head", split_axis=1, concat_axis=1, tiled=True)
    return jnp.sum(received.astype(jnp.float32), axis=1)


def block_setup(x_arg, b_arg, decay_arg, resets):
    tokens_here = x_arg.shape[0]
    heads_here = decay_arg.shape[0]
    groups_here = b_arg.shape[1] // N
    x_heads = x_arg.reshape(tokens_here, heads_here, P_SIZE)
    b_groups = b_arg.reshape(tokens_here, groups_here, N)
    cumul = jnp.cumsum(decay_arg, axis=1)
    counts = jnp.cumsum(resets)
    return x_heads, b_groups, cumul, counts, heads_here // groups_here


def block_outputs(x_arg, b_arg, c_arg, decay_arg, resets):
    x_heads, b_groups, cumul, counts, repeat_count = block_setup(x_arg, b_arg, decay_arg, resets)
    tokens_here = x_arg.shape[0]
    c_groups = c_arg.reshape(tokens_here, b_groups.shape[1], N)
    order = jnp.arange(tokens_here, dtype=jnp.int32)
    lower = order[None, :] <= order[:, None]
    same = lower & (counts[:, None] == counts[None, :])
    spread = cumul[:, :, None] - cumul[:, None, :]
    weights = jnp.where(same[None], jnp.exp(jnp.minimum(spread, 0.0)), 0.0)
    scores = jnp.einsum("tgn,sgn->gts", c_groups, b_groups, precision=lax.Precision.HIGH)
    scores = jnp.repeat(scores, repeat_count, axis=0) * weights
    inner = jnp.einsum("hts,shp->thp", scores, x_heads, precision=lax.Precision.HIGH)
    return inner.reshape(tokens_here, -1)


def block_final(x_arg, b_arg, decay_arg, resets):
    x_heads, b_groups, cumul, counts, repeat_count = block_setup(x_arg, b_arg, decay_arg, resets)
    tail = jnp.exp(cumul[:, -1:] - cumul) * (counts == counts[-1]).astype(jnp.float32)[None, :]
    b_heads = jnp.repeat(b_groups, repeat_count, axis=1)
    return jnp.einsum(
        "shp,shn->hpn", x_heads * tail.T[:, :, None], b_heads, precision=lax.Precision.HIGH
    )


def gated_norm(values, gate, gain):
    gated = values * jax.nn.silu(gate)
    rows_here, width = gated.shape
    group_width = HP // G
    grouped = gated.reshape(rows_here, width // group_width, group_width)
    scale = lax.rsqrt(jnp.mean(grouped * grouped, axis=2, keepdims=True) + 1e-05)
    return (grouped * scale).reshape(rows_here, width) * gain[None, :]


def carried_term(inputs_c, log_decay, resets, state):
    heads_here = log_decay.shape[0]
    tokens_here = inputs_c.shape[0]
    groups_here = inputs_c.shape[1] // N
    cumul = jnp.cumsum(log_decay, axis=1)
    counts = jnp.cumsum(resets)
    entry = jnp.exp(cumul) * (counts == 0).astype(jnp.float32)[None, :]
    c_heads = jnp.repeat(
        inputs_c.reshape(tokens_here, groups_here, N), heads_here // groups_here, axis=1
    )
    result = (
        jnp.einsum("thn,hpn->thp", c_heads, state, precision=lax.Precision.HIGH)
        * entry.T[:, :, None]
    )
    return result.reshape(tokens_here, heads_here * P_SIZE)


def device_decay(log_decay, resets):
    return jnp.exp(jnp.sum(log_decay, axis=1)) * (jnp.sum(resets) == 0).astype(jnp.float32)


def per_device(
    inputs_x, inputs_b, inputs_c, gate_z, log_decay, resets, norm_gain, out_weight, out_grad
):
    x_float = inputs_x.astype(jnp.float32)
    b_float = inputs_b.astype(jnp.float32)
    c_float = inputs_c.astype(jnp.float32)
    z_float = gate_z.astype(jnp.float32)
    heads_here = log_decay.shape[0]

    assert inputs_x.shape[0] == SPAN

    def local_outputs(x_arg, b_arg, c_arg, decay_arg):
        return block_outputs(x_arg, b_arg, c_arg, decay_arg, resets)

    def local_final(x_arg, b_arg, decay_arg):
        return block_final(x_arg, b_arg, decay_arg, resets)

    y_zero, pull_outputs = jax.vjp(local_outputs, x_float, b_float, c_float, log_decay)
    s_local, pull_final = jax.vjp(local_final, x_float, b_float, log_decay)

    def whole_decay(decay_arg):
        return device_decay(decay_arg, resets)

    g_local, pull_decay = jax.vjp(whole_decay, log_decay)

    state_in = prefix_combine(g_local, s_local, 1)

    def finish(y_arg, c_arg, decay_arg, z_arg, state_arg):
        return gated_norm(
            y_arg + carried_term(c_arg, decay_arg, resets, state_arg), z_arg, norm_gain
        )

    normed, pull_finish = jax.vjp(finish, y_zero, c_float, log_decay, z_float, state_in)
    normed_bf = normed.astype(jnp.bfloat16)
    full_weight = lax.all_gather(out_weight, "seq", axis=0, tiled=True)
    partial_value = lax.dot_general(
        normed_bf, full_weight, (((1,), (1,)), ((), ())), preferred_element_type=jnp.float32
    )
    layer_out = head_sum_scatter(partial_value.astype(jnp.bfloat16)).astype(jnp.bfloat16)
    grad_full = head_gather(out_grad)
    grad_y = jnp.dot(grad_full, full_weight, preferred_element_type=jnp.float32)
    seq_count = lax.axis_size("seq")
    weight_term = lax.dot_general(
        grad_full, normed_bf, (((0,), (0,)), ((), ())), preferred_element_type=jnp.float32
    ).astype(jnp.bfloat16)
    weight_blocks = lax.all_to_all(
        weight_term.reshape(seq_count, -1, weight_term.shape[1]),
        "seq",
        split_axis=0,
        concat_axis=0,
        tiled=True,
    )
    grad_weight = jnp.sum(weight_blocks.astype(jnp.float32), axis=0)
    d_zero, d_c_two, d_decay_two, grad_z, adjoint_in = pull_finish(grad_y)

    adjoint_out = prefix_combine(g_local, adjoint_in, -1)
    x_one, b_one, d_c_one, decay_one = pull_outputs(d_zero)
    x_two, b_two, decay_two = pull_final(adjoint_out)
    grad_x = x_one + x_two
    grad_b = b_one + b_two
    d_decay_one = decay_one + decay_two
    (d_decay_three,) = pull_decay(jnp.sum(adjoint_out * state_in, axis=(1, 2)))
    return (
        layer_out,
        grad_x,
        grad_b,
        d_c_one + d_c_two,
        grad_z,
        d_decay_one + d_decay_two + d_decay_three,
        grad_weight,
    )


def solution(mesh):
    return jax.shard_map(
        per_device,
        mesh=mesh,
        in_specs=(
            P("seq", "head"),
            P("seq", "head"),
            P("seq", "head"),
            P("seq", "head"),
            P("head", "seq"),
            P("seq"),
            P("head"),
            P("seq", "head"),
            P("seq", "head"),
        ),
        out_specs=(
            P("seq", "head"),
            P("seq", "head"),
            P("seq", "head"),
            P("seq", "head"),
            P("seq", "head"),
            P("head", "seq"),
            P("seq", "head"),
        ),
        check_vma=False,
    )
```

```python
import jax
import jax.numpy as jnp
from jax import lax
from jax.sharding import PartitionSpec as P

P_SIZE = 64
N = 128
G = 8
SPAN = 256
HP = 8192


def from_behind(value, axis, steps):
    count = lax.axis_size(axis)
    leading, last = (max(0, -steps), min(count, count - steps))
    return lax.ppermute(value, axis, [(source, source + steps) for source in range(leading, last)])


def with_decay(state, decay):
    high = decay.astype(jnp.bfloat16)
    low = (decay - high.astype(jnp.float32)).astype(jnp.bfloat16)
    rows = jnp.zeros((state.shape[0], 8, state.shape[2]), jnp.bfloat16)
    rows = rows.at[:, 0, :].set(high[:, None]).at[:, 1, :].set(low[:, None])
    return jnp.concatenate([state.astype(jnp.bfloat16), rows], axis=1)


def split_decay(payload, rows):
    state = payload[:, :rows].astype(jnp.float32)
    decay = payload[:, rows, 0].astype(jnp.float32) + payload[:, rows + 1, 0].astype(jnp.float32)
    return state, decay


def prefix_combine(decay, value, direction, width=4):
    count = lax.axis_size("seq")
    rows = value.shape[1]

    def shifted(payload, steps):
        return split_decay(from_behind(payload, "seq", direction * steps), rows)

    near = min(width, count - 1)
    outgoing = with_decay(value, decay)
    total, passed = shifted(outgoing, 1)
    for steps in range(2, near + 1):
        item, item_decay = shifted(outgoing, steps)
        total = total + passed[:, None, None] * item
        passed = passed * item_decay
    result = total
    outgoing = with_decay(total, passed)
    through = passed
    for steps in range(near, count - 1, near):
        item, item_decay = shifted(outgoing, steps)
        result = result + through[:, None, None] * item
        through = through * item_decay
    return result


def head_gather(block):
    count = lax.axis_size("head")
    rows, width = block.shape
    copies = jnp.broadcast_to(block[:, None, :], (rows, count, width))
    gathered = lax.all_to_all(copies, "head", split_axis=1, concat_axis=1, tiled=True)
    return gathered.reshape(rows, count * width)


def head_sum_scatter(full):
    count = lax.axis_size("head")
    rows = full.shape[0]
    pieces = full.reshape(rows, count, -1)
    received = lax.all_to_all(pieces, "head", split_axis=1, concat_axis=1, tiled=True)
    return jnp.sum(received.astype(jnp.float32), axis=1)


def block_setup(x_arg, b_arg, decay_arg, resets):
    tokens_here = x_arg.shape[0]
    heads_here = decay_arg.shape[0]
    groups_here = b_arg.shape[1] // N
    x_heads = x_arg.reshape(tokens_here, heads_here, P_SIZE)
    b_groups = b_arg.reshape(tokens_here, groups_here, N)
    cumul = jnp.cumsum(decay_arg, axis=1)
    counts = jnp.cumsum(resets)
    return x_heads, b_groups, cumul, counts, heads_here // groups_here


def block_outputs(x_arg, b_arg, c_arg, decay_arg, resets):
    x_heads, b_groups, cumul, counts, repeat_count = block_setup(x_arg, b_arg, decay_arg, resets)
    tokens_here = x_arg.shape[0]
    c_groups = c_arg.reshape(tokens_here, b_groups.shape[1], N)
    order = jnp.arange(tokens_here, dtype=jnp.int32)
    lower = order[None, :] <= order[:, None]
    same = lower & (counts[:, None] == counts[None, :])
    spread = cumul[:, :, None] - cumul[:, None, :]
    weights = jnp.where(same[None], jnp.exp(jnp.minimum(spread, 0.0)), 0.0)
    scores = jnp.einsum("tgn,sgn->gts", c_groups, b_groups, precision=lax.Precision.HIGH)
    scores = jnp.repeat(scores, repeat_count, axis=0) * weights
    inner = jnp.einsum("hts,shp->thp", scores, x_heads, precision=lax.Precision.HIGH)
    return inner.reshape(tokens_here, -1)


def block_final(x_arg, b_arg, decay_arg, resets):
    x_heads, b_groups, cumul, counts, repeat_count = block_setup(x_arg, b_arg, decay_arg, resets)
    tail = jnp.exp(cumul[:, -1:] - cumul) * (counts == counts[-1]).astype(jnp.float32)[None, :]
    b_heads = jnp.repeat(b_groups, repeat_count, axis=1)
    return jnp.einsum(
        "shp,shn->hpn", x_heads * tail.T[:, :, None], b_heads, precision=lax.Precision.HIGH
    )


def gated_norm(values, gate, gain):
    gated = values * jax.nn.silu(gate)
    rows_here, width = gated.shape
    group_width = HP // G
    grouped = gated.reshape(rows_here, width // group_width, group_width)
    scale = lax.rsqrt(jnp.mean(grouped * grouped, axis=2, keepdims=True) + 1e-05)
    return (grouped * scale).reshape(rows_here, width) * gain[None, :]


def carried_term(inputs_c, log_decay, resets, state):
    heads_here = log_decay.shape[0]
    tokens_here = inputs_c.shape[0]
    groups_here = inputs_c.shape[1] // N
    cumul = jnp.cumsum(log_decay, axis=1)
    counts = jnp.cumsum(resets)
    entry = jnp.exp(cumul) * (counts == 0).astype(jnp.float32)[None, :]
    c_heads = jnp.repeat(
        inputs_c.reshape(tokens_here, groups_here, N), heads_here // groups_here, axis=1
    )
    result = (
        jnp.einsum("thn,hpn->thp", c_heads, state, precision=lax.Precision.HIGH)
        * entry.T[:, :, None]
    )
    return result.reshape(tokens_here, heads_here * P_SIZE)


def device_decay(log_decay, resets):
    return jnp.exp(jnp.sum(log_decay, axis=1)) * (jnp.sum(resets) == 0).astype(jnp.float32)


def per_device(
    inputs_x, inputs_b, inputs_c, gate_z, log_decay, resets, norm_gain, out_weight, out_grad
):
    x_float = inputs_x.astype(jnp.float32)
    b_float = inputs_b.astype(jnp.float32)
    c_float = inputs_c.astype(jnp.float32)
    z_float = gate_z.astype(jnp.float32)

    assert inputs_x.shape[0] == SPAN

    def local_outputs(x_arg, b_arg, c_arg, decay_arg):
        return block_outputs(x_arg, b_arg, c_arg, decay_arg, resets)

    def local_final(x_arg, b_arg, decay_arg):
        return block_final(x_arg, b_arg, decay_arg, resets)

    y_zero, pull_outputs = jax.vjp(local_outputs, x_float, b_float, c_float, log_decay)
    s_local, pull_final = jax.vjp(local_final, x_float, b_float, log_decay)

    def whole_decay(decay_arg):
        return device_decay(decay_arg, resets)

    g_local, pull_decay = jax.vjp(whole_decay, log_decay)

    state_in = prefix_combine(g_local, s_local, 1)

    def finish(y_arg, c_arg, decay_arg, z_arg, state_arg):
        return gated_norm(
            y_arg + carried_term(c_arg, decay_arg, resets, state_arg), z_arg, norm_gain
        )

    normed, pull_finish = jax.vjp(finish, y_zero, c_float, log_decay, z_float, state_in)
    normed_bf = normed.astype(jnp.bfloat16)
    full_weight = lax.all_gather(out_weight, "seq", axis=0, tiled=True)
    partial_value = lax.dot_general(
        normed_bf, full_weight, (((1,), (1,)), ((), ())), preferred_element_type=jnp.float32
    )
    layer_out = head_sum_scatter(partial_value.astype(jnp.bfloat16)).astype(jnp.bfloat16)
    grad_full = head_gather(out_grad)
    weight_term = lax.dot_general(
        grad_full, normed_bf, (((0,), (0,)), ((), ())), preferred_element_type=jnp.float32
    ).astype(jnp.bfloat16)
    grad_weight = lax.psum_scatter(
        weight_term, "seq", scatter_dimension=0, tiled=True
    ).astype(jnp.float32)
    after_term = grad_full + weight_term[0, 0] * jnp.zeros((), jnp.bfloat16)
    grad_y = jnp.dot(after_term, full_weight, preferred_element_type=jnp.float32)
    d_zero, d_c_two, d_decay_two, grad_z, adjoint_in = pull_finish(grad_y)

    adjoint_out = prefix_combine(g_local, adjoint_in, -1)
    x_one, b_one, d_c_one, decay_one = pull_outputs(d_zero)
    x_two, b_two, decay_two = pull_final(adjoint_out)
    grad_x = x_one + x_two
    grad_b = b_one + b_two
    d_decay_one = decay_one + decay_two
    (d_decay_three,) = pull_decay(jnp.sum(adjoint_out * state_in, axis=(1, 2)))
    return (
        layer_out,
        grad_x,
        grad_b,
        d_c_one + d_c_two,
        grad_z,
        d_decay_one + d_decay_two + d_decay_three,
        grad_weight,
    )


def solution(mesh):
    return jax.shard_map(
        per_device,
        mesh=mesh,
        in_specs=(
            P("seq", "head"),
            P("seq", "head"),
            P("seq", "head"),
            P("seq", "head"),
            P("head", "seq"),
            P("seq"),
            P("head"),
            P("seq", "head"),
            P("seq", "head"),
        ),
        out_specs=(
            P("seq", "head"),
            P("seq", "head"),
            P("seq", "head"),
            P("seq", "head"),
            P("seq", "head"),
            P("head", "seq"),
            P("seq", "head"),
        ),
        check_vma=False,
    )
```

```python
import jax
import jax.numpy as jnp
from jax import lax
from jax.sharding import PartitionSpec as P

P_SIZE = 64
N = 128
G = 8
SPAN = 256
HP = 8192


def from_behind(value, axis, steps):
    count = lax.axis_size(axis)
    leading, last = (max(0, -steps), min(count, count - steps))
    return lax.ppermute(value, axis, [(source, source + steps) for source in range(leading, last)])


def with_decay(state, decay):
    high = decay.astype(jnp.bfloat16)
    low = (decay - high.astype(jnp.float32)).astype(jnp.bfloat16)
    rows = jnp.zeros((state.shape[0], 8, state.shape[2]), jnp.bfloat16)
    rows = rows.at[:, 0, :].set(high[:, None]).at[:, 1, :].set(low[:, None])
    return jnp.concatenate([state.astype(jnp.bfloat16), rows], axis=1)


def split_decay(payload, rows):
    state = payload[:, :rows].astype(jnp.float32)
    decay = payload[:, rows, 0].astype(jnp.float32) + payload[:, rows + 1, 0].astype(jnp.float32)
    return state, decay


def prefix_combine(decay, value, direction, width=4):
    count = lax.axis_size("seq")
    rows = value.shape[1]

    def shifted(payload, steps):
        return split_decay(from_behind(payload, "seq", direction * steps), rows)

    near = min(width, count - 1)
    outgoing = with_decay(value, decay)
    total, passed = shifted(outgoing, 1)
    for steps in range(2, near + 1):
        item, item_decay = shifted(outgoing, steps)
        total = total + passed[:, None, None] * item
        passed = passed * item_decay
    result = total
    outgoing = with_decay(total, passed)
    through = passed
    for steps in range(near, count - 1, near):
        item, item_decay = shifted(outgoing, steps)
        result = result + through[:, None, None] * item
        through = through * item_decay
    return result


def head_gather(block):
    count = lax.axis_size("head")
    rows, width = block.shape
    copies = jnp.broadcast_to(block[:, None, :], (rows, count, width))
    gathered = lax.all_to_all(copies, "head", split_axis=1, concat_axis=1, tiled=True)
    return gathered.reshape(rows, count * width)


def head_sum_scatter(full):
    count = lax.axis_size("head")
    rows = full.shape[0]
    pieces = full.reshape(rows, count, -1)
    received = lax.all_to_all(pieces, "head", split_axis=1, concat_axis=1, tiled=True)
    return jnp.sum(received.astype(jnp.float32), axis=1)


def block_setup(x_arg, b_arg, decay_arg, resets):
    tokens_here = x_arg.shape[0]
    heads_here = decay_arg.shape[0]
    groups_here = b_arg.shape[1] // N
    x_heads = x_arg.reshape(tokens_here, heads_here, P_SIZE)
    b_groups = b_arg.reshape(tokens_here, groups_here, N)
    cumul = jnp.cumsum(decay_arg, axis=1)
    counts = jnp.cumsum(resets)
    return x_heads, b_groups, cumul, counts, heads_here // groups_here


def block_outputs(x_arg, b_arg, c_arg, decay_arg, resets):
    x_heads, b_groups, cumul, counts, repeat_count = block_setup(x_arg, b_arg, decay_arg, resets)
    tokens_here = x_arg.shape[0]
    c_groups = c_arg.reshape(tokens_here, b_groups.shape[1], N)
    order = jnp.arange(tokens_here, dtype=jnp.int32)
    lower = order[None, :] <= order[:, None]
    same = lower & (counts[:, None] == counts[None, :])
    spread = cumul[:, :, None] - cumul[:, None, :]
    weights = jnp.where(same[None], jnp.exp(jnp.minimum(spread, 0.0)), 0.0)
    scores = jnp.einsum("tgn,sgn->gts", c_groups, b_groups, precision=lax.Precision.HIGH)
    scores = jnp.repeat(scores, repeat_count, axis=0) * weights
    inner = jnp.einsum("hts,shp->thp", scores, x_heads, precision=lax.Precision.HIGH)
    return inner.reshape(tokens_here, -1)


def block_final(x_arg, b_arg, decay_arg, resets):
    x_heads, b_groups, cumul, counts, repeat_count = block_setup(x_arg, b_arg, decay_arg, resets)
    tail = jnp.exp(cumul[:, -1:] - cumul) * (counts == counts[-1]).astype(jnp.float32)[None, :]
    b_heads = jnp.repeat(b_groups, repeat_count, axis=1)
    return jnp.einsum(
        "shp,shn->hpn", x_heads * tail.T[:, :, None], b_heads, precision=lax.Precision.HIGH
    )


def gated_norm(values, gate, gain):
    gated = values * jax.nn.silu(gate)
    rows_here, width = gated.shape
    group_width = HP // G
    grouped = gated.reshape(rows_here, width // group_width, group_width)
    scale = lax.rsqrt(jnp.mean(grouped * grouped, axis=2, keepdims=True) + 1e-05)
    return (grouped * scale).reshape(rows_here, width) * gain[None, :]


def carried_term(inputs_c, log_decay, resets, state):
    heads_here = log_decay.shape[0]
    tokens_here = inputs_c.shape[0]
    groups_here = inputs_c.shape[1] // N
    cumul = jnp.cumsum(log_decay, axis=1)
    counts = jnp.cumsum(resets)
    entry = jnp.exp(cumul) * (counts == 0).astype(jnp.float32)[None, :]
    c_heads = jnp.repeat(
        inputs_c.reshape(tokens_here, groups_here, N), heads_here // groups_here, axis=1
    )
    result = (
        jnp.einsum("thn,hpn->thp", c_heads, state, precision=lax.Precision.HIGH)
        * entry.T[:, :, None]
    )
    return result.reshape(tokens_here, heads_here * P_SIZE)


def device_decay(log_decay, resets):
    return jnp.exp(jnp.sum(log_decay, axis=1)) * (jnp.sum(resets) == 0).astype(jnp.float32)


def per_device(
    inputs_x, inputs_b, inputs_c, gate_z, log_decay, resets, norm_gain, out_weight, out_grad
):
    x_float = inputs_x.astype(jnp.float32)
    b_float = inputs_b.astype(jnp.float32)
    c_float = inputs_c.astype(jnp.float32)
    z_float = gate_z.astype(jnp.float32)

    assert inputs_x.shape[0] == SPAN

    def local_outputs(x_arg, b_arg, c_arg, decay_arg):
        return block_outputs(x_arg, b_arg, c_arg, decay_arg, resets)

    def local_final(x_arg, b_arg, decay_arg):
        return block_final(x_arg, b_arg, decay_arg, resets)

    y_zero, pull_outputs = jax.vjp(local_outputs, x_float, b_float, c_float, log_decay)
    s_local, pull_final = jax.vjp(local_final, x_float, b_float, log_decay)

    def whole_decay(decay_arg):
        return device_decay(decay_arg, resets)

    g_local, pull_decay = jax.vjp(whole_decay, log_decay)

    state_in = prefix_combine(g_local, s_local, 1)

    def finish(y_arg, c_arg, decay_arg, z_arg, state_arg):
        return gated_norm(
            y_arg + carried_term(c_arg, decay_arg, resets, state_arg), z_arg, norm_gain
        )

    normed, pull_finish = jax.vjp(finish, y_zero, c_float, log_decay, z_float, state_in)
    normed_bf = normed.astype(jnp.bfloat16)
    full_weight = lax.all_gather(out_weight, "seq", axis=0, tiled=True)
    partial_value = lax.dot_general(
        normed_bf, full_weight, (((1,), (1,)), ((), ())), preferred_element_type=jnp.float32
    )
    layer_out = head_sum_scatter(partial_value.astype(jnp.bfloat16)).astype(jnp.bfloat16)
    grad_full = head_gather(out_grad)
    weight_term = lax.dot_general(
        grad_full, normed_bf, (((0,), (0,)), ((), ())), preferred_element_type=jnp.float32
    ).astype(jnp.bfloat16)
    seq_count = lax.axis_size("seq")
    parity = lax.axis_index("seq") % 2
    blocks = weight_term.reshape(seq_count // 2, 2, -1, weight_term.shape[1])
    mine = lax.dynamic_index_in_dim(blocks, parity, axis=1, keepdims=False)
    theirs = lax.dynamic_index_in_dim(blocks, 1 - parity, axis=1, keepdims=False)
    partner = lax.ppermute(theirs, "seq", [(peer, peer ^ 1) for peer in range(seq_count)])
    pair_sum = (mine.astype(jnp.float32) + partner.astype(jnp.float32)).astype(jnp.bfloat16)
    groups = [list(range(start, seq_count, 2)) for start in range(2)]
    grad_weight = lax.psum_scatter(
        pair_sum.reshape(-1, weight_term.shape[1]),
        "seq",
        scatter_dimension=0,
        tiled=True,
        axis_index_groups=groups,
    ).astype(jnp.float32)
    after_term = grad_full + weight_term[0, 0] * jnp.zeros((), jnp.bfloat16)
    grad_y = jnp.dot(after_term, full_weight, preferred_element_type=jnp.float32)
    d_zero, d_c_two, d_decay_two, grad_z, adjoint_in = pull_finish(grad_y)

    adjoint_out = prefix_combine(g_local, adjoint_in, -1)
    x_one, b_one, d_c_one, decay_one = pull_outputs(d_zero)
    x_two, b_two, decay_two = pull_final(adjoint_out)
    grad_x = x_one + x_two
    grad_b = b_one + b_two
    d_decay_one = decay_one + decay_two
    (d_decay_three,) = pull_decay(jnp.sum(adjoint_out * state_in, axis=(1, 2)))
    return (
        layer_out,
        grad_x,
        grad_b,
        d_c_one + d_c_two,
        grad_z,
        d_decay_one + d_decay_two + d_decay_three,
        grad_weight,
    )


def solution(mesh):
    return jax.shard_map(
        per_device,
        mesh=mesh,
        in_specs=(
            P("seq", "head"),
            P("seq", "head"),
            P("seq", "head"),
            P("seq", "head"),
            P("head", "seq"),
            P("seq"),
            P("head"),
            P("seq", "head"),
            P("seq", "head"),
        ),
        out_specs=(
            P("seq", "head"),
            P("seq", "head"),
            P("seq", "head"),
            P("seq", "head"),
            P("seq", "head"),
            P("head", "seq"),
            P("seq", "head"),
        ),
        check_vma=False,
    )
```
